256 devices in a mesh: lon: 16 (over x, y_lo, core), lat: 16 (over y_hi, z).
Axes of the slice: x: 4, y: 4 (y_hi: 2, y_lo: 2; y = y_hi * 2 + y_lo), z: 8, core: 2. Of those that a mesh axis runs over, the one named last changes fastest.
Arguments:
- height: float32 [3072, 7200], P('lat', 'lon'), may hold values from 0.4 to 1.6
- east_wind: float32 [3072, 7200], P('lat', 'lon'), may hold values from -1.5 to 1.5
- north_wind: float32 [3072, 7200], P('lat', 'lon'), may hold values from -1.5 to 1.5
- cutoffs: int32 [512], replicated, may hold values from 1 to 64
Outputs:
- height_final: float32 [3072, 7200], P('lat', 'lon')
- east_final: float32 [3072, 7200], P('lat', 'lon')
- north_final: float32 [3072, 7200], P('lat', 'lon')
The draws below stay inside these ranges and needn't reach their ends.
All inputs are finite; a program needn't handle non-finite values.
Results may differ from the reference program's by a relative error of at most 0.0002.
Values sent between devices are 32-bit elements; how exact they have to be, the bound alone decides.
No kernel may reach another device: no remote copies, remote signals or barrier semaphores. Data moves between devices by JAX's collectives and lax.ppermute only.
A program may use at most 128 MiB of HBM per device.

```python
import math
import jax
import jax.numpy as jnp

NLON = 7200
LAT_ROWS = 3600
KMAX = 64
STEPS = 2
ROWS = 3072
FROWS = 512


def cutoff_rows(key):
    rows = jnp.arange(FROWS, dtype=jnp.int32)
    jitter = jax.random.randint(jax.random.fold_in(key, 11), (FROWS,), 0, 3) * (rows > 0).astype(jnp.int32)
    return jnp.minimum(KMAX, 1 + rows * KMAX // FROWS + jitter).astype(jnp.int32)


def draw_cutoffs(key, part):
    return cutoff_rows(key)


def wave_field(key, salt, middle, rough, wave):
    cutoff = cutoff_rows(key)
    rows = jnp.arange(ROWS, dtype=jnp.int32)
    polar = rows < FROWS
    polar_share = polar.astype(jnp.float32)
    ceiling = jnp.where(polar, cutoff[jnp.minimum(rows, FROWS - 1)], KMAX)
    keys = jax.random.split(jax.random.fold_in(key, salt), 10)
    modes = jax.random.randint(keys[0], (ROWS, 4), 1, ceiling[:, None] + 1)
    offsets = jax.random.randint(keys[1], (ROWS, 4), 0, NLON)
    upper = jnp.minimum(2 * ceiling + 2, NLON // 2)
    extra_modes = jax.random.randint(keys[6], (ROWS, 2), ceiling[:, None] + 1, upper[:, None])
    extra_offsets = jax.random.randint(keys[7], (ROWS, 2), 0, NLON)
    columns = jnp.arange(NLON, dtype=jnp.int32)
    amounts = jax.random.uniform(keys[3], (ROWS, 4), minval=-wave, maxval=wave)
    noise = jax.random.uniform(keys[5], (ROWS, NLON), minval=-rough, maxval=rough)
    extra_amounts = jax.random.uniform(keys[9], (ROWS, 2), minval=-0.5 * rough, maxval=0.5 * rough)
    total = middle + noise * (1.0 - polar_share)[:, None]
    for term in range(2):
        turn = extra_modes[:, term:term + 1] * (columns[None, :] + extra_offsets[:, term:term + 1]) % NLON
        total = total + polar_share[:, None] * extra_amounts[:, term:term + 1] * jnp.cos(turn.astype(jnp.float32) * (2.0 * math.pi / NLON))
    for term in range(4):
        turn = modes[:, term:term + 1] * (columns[None, :] + offsets[:, term:term + 1]) % NLON
        total = total + amounts[:, term:term + 1] * jnp.cos(turn.astype(jnp.float32) * (2.0 * math.pi / NLON))
    return total.astype(jnp.float32)


def draw_height(key, part):
    return wave_field(key, 21, 1.0, 0.2, 0.1)


def draw_east_wind(key, part):
    return wave_field(key, 22, 0.0, 0.3, 0.3)


def draw_north_wind(key, part):
    return wave_field(key, 23, 0.0, 0.3, 0.3)


def setup_inputs(seed: int = 0) -> dict:
    streams_of = jax.random.split(jax.random.key(seed), 5)
    height = draw_height(jax.random.fold_in(streams_of[4], 71), 0)
    east_wind = draw_east_wind(jax.random.fold_in(streams_of[4], 71), 0)
    north_wind = draw_north_wind(jax.random.fold_in(streams_of[4], 71), 0)
    cutoffs = draw_cutoffs(jax.random.fold_in(streams_of[4], 71), 0)
    return {"height": height, "east_wind": east_wind, "north_wind": north_wind, "cutoffs": cutoffs}


COURANT = 0.1
OMEGA_RATE = 1.5


def zonal_diff(field, lon_step):
    return (jnp.roll(field, -1, axis=1) - jnp.roll(field, 1, axis=1)) * (0.5 / lon_step)


def north_diff(field, lat_step):
    return (field[:-2] - field[2:]) * (0.5 / lat_step)


def extend_rows(field, flip):
    mirror = flip * jnp.roll(field[0:1], NLON // 2, axis=1)
    return jnp.concatenate([mirror, field, field[-1:]], axis=0)


def tendency(state, coslat, sinlat, cos_tall, lon_step, lat_step):
    height, east, north = state
    height_tall = extend_rows(height, 1.0)
    east_tall = extend_rows(east, -1.0)
    north_tall = extend_rows(north, -1.0)
    inv_cos = 1.0 / coslat
    turning = 2.0 * OMEGA_RATE * sinlat + east * sinlat * inv_cos
    rate_height = -(zonal_diff(height * east, lon_step) + north_diff(height_tall * north_tall * cos_tall, lat_step)) * inv_cos
    rate_east = -east * zonal_diff(east, lon_step) * inv_cos - north * north_diff(east_tall, lat_step) + turning * north - zonal_diff(height, lon_step) * inv_cos
    rate_north = -east * zonal_diff(north, lon_step) * inv_cos - north * north_diff(north_tall, lat_step) - turning * east - north_diff(height_tall, lat_step)
    return (rate_height, rate_east, rate_north)


def polar_filter(field, cutoffs):
    top = field[:FROWS]
    spectrum = jnp.fft.rfft(top, axis=1)
    waves = jnp.arange(NLON // 2 + 1, dtype=jnp.int32)
    keep = waves[None, :] <= cutoffs[:, None]
    low = jnp.fft.irfft(jnp.where(keep, spectrum, 0.0), n=NLON, axis=1).astype(jnp.float32)
    return jnp.concatenate([low, field[FROWS:]], axis=0)


def reference(height, east_wind, north_wind, cutoffs):
    lat_step = math.pi / LAT_ROWS
    lon_step = 2.0 * math.pi / NLON
    time_step = COURANT * lat_step
    index = jnp.arange(-1, ROWS + 1).astype(jnp.float32)
    cos_all = jnp.abs(jnp.sin((index + 0.5) * lat_step))
    sin_all = jnp.cos((index + 0.5) * lat_step)
    coslat = cos_all[1:-1][:, None]
    sinlat = sin_all[1:-1][:, None]
    cos_tall = cos_all[:, None]
    state = (height, east_wind, north_wind)
    for step_index in range(STEPS):
        rates = tendency(state, coslat, sinlat, cos_tall, lon_step, lat_step)
        middle = tuple(field + (0.5 * time_step) * rate for field, rate in zip(state, rates))
        rates = tendency(middle, coslat, sinlat, cos_tall, lon_step, lat_step)
        state = tuple(polar_filter(field + time_step * rate, cutoffs) for field, rate in zip(state, rates))
    return (state[0], state[1], state[2])
```

```python
import math

import jax
import jax.numpy as jnp
from jax import lax
from jax.sharding import PartitionSpec as P

NLON = 7200
LAT_ROWS = 3600
KMAX = 64
STEPS = 2


COURANT = 0.1
OMEGA_RATE = 1.5


def with_halo(value, sides, width, wrap):
    for axis, dim in sides:
        devices, length = (lax.axis_size(axis), value.shape[dim])
        up = [(i, (i + 1) % devices) for i in range(devices if wrap else devices - 1)]
        down = [(j, i) for i, j in up]
        last = lax.slice_in_dim(value, length - width, length, axis=dim)
        first = lax.slice_in_dim(value, 0, width, axis=dim)
        before = lax.ppermute(last, axis, up)
        after = lax.ppermute(first, axis, down)
        value = jnp.concatenate([before, value, after], axis=dim)
    return value


def from_behind(value, axis, by):
    devices = lax.axis_size(axis)
    return lax.ppermute(value, axis, [(i, (i + by) % devices) for i in range(devices)])


def local_table(width):
    waves = jnp.arange(KMAX + 1, dtype=jnp.int32)
    columns = lax.axis_index("lon") * width + jnp.arange(width, dtype=jnp.int32)
    phase = waves[:, None] * columns[None, :] % NLON
    angle = phase.astype(jnp.float32) * (2.0 * math.pi / NLON)
    return jnp.concatenate([jnp.cos(angle), jnp.sin(angle)], axis=0)


def spectral_weights(cut_rows):
    waves = jnp.arange(KMAX + 1, dtype=jnp.int32)
    scale = jnp.where(waves == 0, 1.0 / NLON, 2.0 / NLON).astype(jnp.float32)
    keep = (waves[None, :] <= cut_rows[:, None]).astype(jnp.float32) * scale[None, :]
    return jnp.concatenate([keep, keep], axis=1)


def project(fields, table):
    return jnp.einsum("fnw,kw->fnk", fields, table, precision=lax.Precision.HIGHEST)


def expand(coeffs, table):
    return jnp.einsum("fnk,kw->fnw", coeffs, table, precision=lax.Precision.HIGHEST)


def low_pass(fields, cut_rows, active, table):
    weights = spectral_weights(cut_rows)
    coeffs = lax.psum(project(fields, table), "lon") * weights[None]
    smooth = expand(coeffs, table)
    return jnp.where(active[None, :, None], smooth, fields)


def filter_state(state, cutoffs, table):
    rows_here = state.shape[1]
    lat_count = lax.axis_size("lat")
    lat_index = lax.axis_index("lat")
    filtered_rows = cutoffs.shape[0]
    cut_all = jnp.pad(cutoffs, (0, rows_here * lat_count - filtered_rows))
    global_rows = lat_index * rows_here + jnp.arange(rows_here, dtype=jnp.int32)
    cut_rows = lax.dynamic_slice_in_dim(cut_all, lat_index * rows_here, rows_here, 0)
    return low_pass(state, cut_rows, global_rows < filtered_rows, table)


def tendency(state, cos_all, sinlat, lon_step, lat_step):
    lat_index = lax.axis_index("lat")
    lat_count = lax.axis_size("lat")
    edge_cols = jnp.concatenate([state[:, :, :1], state[:, :, -1:]], axis=2)
    got_cols = with_halo(edge_cols, (("lon", 2),), 1, True)
    west_col = got_cols[:, :, 0:1]
    east_col = got_cols[:, :, 3:4]
    edge_rows = jnp.concatenate([state[:, :1, :], state[:, -1:, :]], axis=1)
    got_rows = with_halo(edge_rows, (("lat", 1),), 1, False)
    flips = jnp.array([1.0, -1.0, -1.0], jnp.float32)
    mirror = from_behind(state[:, 0, :], "lon", lax.axis_size("lon") // 2) * flips[:, None]
    northmost = jnp.where(lat_index == 0, mirror, got_rows[:, 0, :])
    southmost = jnp.where(lat_index == lat_count - 1, state[:, -1, :], got_rows[:, 3, :])
    corner = jnp.zeros((3, 1, 1), jnp.float32)
    top_line = jnp.concatenate([corner, northmost[:, None, :], corner], axis=2)
    bottom_line = jnp.concatenate([corner, southmost[:, None, :], corner], axis=2)
    middle_lines = jnp.concatenate([west_col, state, east_col], axis=2)
    extended = jnp.concatenate([top_line, middle_lines, bottom_line], axis=1)
    east_side = extended[:, 1:-1, 2:]
    west_side = extended[:, 1:-1, :-2]
    north_side = extended[:, :-2, 1:-1]
    south_side = extended[:, 2:, 1:-1]
    cos_north = cos_all[:-2][:, None]
    cos_south = cos_all[2:][:, None]
    coslat = cos_all[1:-1][:, None]

    def zonal_pair(east_value, west_value):
        return (east_value - west_value) * (0.5 / lon_step)

    def north_pair(north_value, south_value):
        return (north_value - south_value) * (0.5 / lat_step)

    height, east, north = (state[0], state[1], state[2])
    inv_cos = 1.0 / coslat
    turning = 2.0 * OMEGA_RATE * sinlat + east * sinlat * inv_cos
    flux_north = north_side[0] * north_side[2] * cos_north
    flux_south = south_side[0] * south_side[2] * cos_south
    rate_height = (
        -(
            zonal_pair(east_side[0] * east_side[1], west_side[0] * west_side[1])
            + north_pair(flux_north, flux_south)
        )
        * inv_cos
    )
    rate_east = (
        -east * zonal_pair(east_side[1], west_side[1]) * inv_cos
        - north * north_pair(north_side[1], south_side[1])
        + turning * north
        - zonal_pair(east_side[0], west_side[0]) * inv_cos
    )
    rate_north = (
        -east * zonal_pair(east_side[2], west_side[2]) * inv_cos
        - north * north_pair(north_side[2], south_side[2])
        - turning * east
        - north_pair(north_side[0], south_side[0])
    )
    return jnp.stack([rate_height, rate_east, rate_north], axis=0)


def shards(height, east_wind, north_wind, cutoffs):
    rows_here = height.shape[0]
    lat_index = lax.axis_index("lat")
    lat_step = math.pi / LAT_ROWS
    lon_step = 2.0 * math.pi / NLON
    time_step = COURANT * lat_step
    first_row = (lat_index * rows_here).astype(jnp.float32)
    index = first_row + jnp.arange(-1, rows_here + 1).astype(jnp.float32)
    cos_all = jnp.abs(jnp.sin((index + 0.5) * lat_step))
    sin_all = jnp.cos((index + 0.5) * lat_step)
    sinlat = sin_all[1:-1][:, None]
    table = local_table(height.shape[1])
    state = jnp.stack([height, east_wind, north_wind], axis=0)
    for step_index in range(STEPS):
        rates = tendency(state, cos_all, sinlat, lon_step, lat_step)
        middle = state + 0.5 * time_step * rates
        rates = tendency(middle, cos_all, sinlat, lon_step, lat_step)
        advanced = state + time_step * rates
        state = filter_state(advanced, cutoffs, table)
    return (state[0], state[1], state[2])


def solution(mesh):
    placed = (P("lat", "lon"), P("lat", "lon"), P("lat", "lon"), P())
    return jax.shard_map(
        shards,
        mesh=mesh,
        in_specs=placed,
        out_specs=(P("lat", "lon"), P("lat", "lon"), P("lat", "lon")),
        check_vma=False,
    )
```

```python
import math

import jax
import jax.numpy as jnp
from jax import lax
from jax.sharding import PartitionSpec as P

NLON = 7200
LAT_ROWS = 3600
KMAX = 64
STEPS = 2


COURANT = 0.1
OMEGA_RATE = 1.5


def with_halo(value, sides, width, wrap):
    for axis, dim in sides:
        devices, length = (lax.axis_size(axis), value.shape[dim])
        up = [(i, (i + 1) % devices) for i in range(devices if wrap else devices - 1)]
        down = [(j, i) for i, j in up]
        last = lax.slice_in_dim(value, length - width, length, axis=dim)
        first = lax.slice_in_dim(value, 0, width, axis=dim)
        before = lax.ppermute(last, axis, up)
        after = lax.ppermute(first, axis, down)
        value = jnp.concatenate([before, value, after], axis=dim)
    return value


def from_behind(value, axis, by):
    devices = lax.axis_size(axis)
    return lax.ppermute(value, axis, [(i, (i + by) % devices) for i in range(devices)])


def local_table(width):
    waves = jnp.arange(KMAX + 1, dtype=jnp.int32)
    columns = lax.axis_index("lon") * width + jnp.arange(width, dtype=jnp.int32)
    phase = waves[:, None] * columns[None, :] % NLON
    angle = phase.astype(jnp.float32) * (2.0 * math.pi / NLON)
    return jnp.concatenate([jnp.cos(angle), jnp.sin(angle)], axis=0)


def spectral_weights(cut_rows):
    waves = jnp.arange(KMAX + 1, dtype=jnp.int32)
    scale = jnp.where(waves == 0, 1.0 / NLON, 2.0 / NLON).astype(jnp.float32)
    keep = (waves[None, :] <= cut_rows[:, None]).astype(jnp.float32) * scale[None, :]
    return jnp.concatenate([keep, keep], axis=1)


def project(fields, table):
    return jnp.einsum("fnw,kw->fnk", fields, table, precision=lax.Precision.HIGHEST)


def expand(coeffs, table):
    return jnp.einsum("fnk,kw->fnw", coeffs, table, precision=lax.Precision.HIGHEST)


def lon_sum(partial):
    devices = lax.axis_size("lon")
    fields, rows, modes = partial.shape
    share = rows // devices
    gathered = lax.all_to_all(partial, "lon", split_axis=1, concat_axis=0, tiled=True)
    reduced = gathered.reshape(devices, fields, share, modes).sum(axis=0)
    copies = jnp.broadcast_to(reduced[None], (devices, fields, share, modes))
    spread = lax.all_to_all(copies, "lon", split_axis=0, concat_axis=2, tiled=True)
    return spread.reshape(fields, rows, modes)


def low_pass(fields, cut_rows, active, table):
    weights = spectral_weights(cut_rows)
    coeffs = lon_sum(project(fields, table)) * weights[None]
    smooth = expand(coeffs, table)
    return jnp.where(active[None, :, None], smooth, fields)


def filter_state(state, cutoffs, table):
    rows_here = state.shape[1]
    lat_count = lax.axis_size("lat")
    lat_index = lax.axis_index("lat")
    filtered_rows = cutoffs.shape[0]
    cut_all = jnp.pad(cutoffs, (0, rows_here * lat_count - filtered_rows))
    global_rows = lat_index * rows_here + jnp.arange(rows_here, dtype=jnp.int32)
    cut_rows = lax.dynamic_slice_in_dim(cut_all, lat_index * rows_here, rows_here, 0)
    return low_pass(state, cut_rows, global_rows < filtered_rows, table)


def tendency(state, cos_all, sinlat, lon_step, lat_step):
    lat_index = lax.axis_index("lat")
    lat_count = lax.axis_size("lat")
    edge_cols = jnp.concatenate([state[:, :, :1], state[:, :, -1:]], axis=2)
    got_cols = with_halo(edge_cols, (("lon", 2),), 1, True)
    west_col = got_cols[:, :, 0:1]
    east_col = got_cols[:, :, 3:4]
    edge_rows = jnp.concatenate([state[:, :1, :], state[:, -1:, :]], axis=1)
    got_rows = with_halo(edge_rows, (("lat", 1),), 1, False)
    flips = jnp.array([1.0, -1.0, -1.0], jnp.float32)
    mirror = from_behind(state[:, 0, :], "lon", lax.axis_size("lon") // 2) * flips[:, None]
    northmost = jnp.where(lat_index == 0, mirror, got_rows[:, 0, :])
    southmost = jnp.where(lat_index == lat_count - 1, state[:, -1, :], got_rows[:, 3, :])
    corner = jnp.zeros((3, 1, 1), jnp.float32)
    top_line = jnp.concatenate([corner, northmost[:, None, :], corner], axis=2)
    bottom_line = jnp.concatenate([corner, southmost[:, None, :], corner], axis=2)
    middle_lines = jnp.concatenate([west_col, state, east_col], axis=2)
    extended = jnp.concatenate([top_line, middle_lines, bottom_line], axis=1)
    east_side = extended[:, 1:-1, 2:]
    west_side = extended[:, 1:-1, :-2]
    north_side = extended[:, :-2, 1:-1]
    south_side = extended[:, 2:, 1:-1]
    cos_north = cos_all[:-2][:, None]
    cos_south = cos_all[2:][:, None]
    coslat = cos_all[1:-1][:, None]

    def zonal_pair(east_value, west_value):
        return (east_value - west_value) * (0.5 / lon_step)

    def north_pair(north_value, south_value):
        return (north_value - south_value) * (0.5 / lat_step)

    height, east, north = (state[0], state[1], state[2])
    inv_cos = 1.0 / coslat
    turning = 2.0 * OMEGA_RATE * sinlat + east * sinlat * inv_cos
    flux_north = north_side[0] * north_side[2] * cos_north
    flux_south = south_side[0] * south_side[2] * cos_south
    rate_height = (
        -(
            zonal_pair(east_side[0] * east_side[1], west_side[0] * west_side[1])
            + north_pair(flux_north, flux_south)
        )
        * inv_cos
    )
    rate_east = (
        -east * zonal_pair(east_side[1], west_side[1]) * inv_cos
        - north * north_pair(north_side[1], south_side[1])
        + turning * north
        - zonal_pair(east_side[0], west_side[0]) * inv_cos
    )
    rate_north = (
        -east * zonal_pair(east_side[2], west_side[2]) * inv_cos
        - north * north_pair(north_side[2], south_side[2])
        - turning * east
        - north_pair(north_side[0], south_side[0])
    )
    return jnp.stack([rate_height, rate_east, rate_north], axis=0)


def shards(height, east_wind, north_wind, cutoffs):
    rows_here = height.shape[0]
    lat_index = lax.axis_index("lat")
    lat_step = math.pi / LAT_ROWS
    lon_step = 2.0 * math.pi / NLON
    time_step = COURANT * lat_step
    first_row = (lat_index * rows_here).astype(jnp.float32)
    index = first_row + jnp.arange(-1, rows_here + 1).astype(jnp.float32)
    cos_all = jnp.abs(jnp.sin((index + 0.5) * lat_step))
    sin_all = jnp.cos((index + 0.5) * lat_step)
    sinlat = sin_all[1:-1][:, None]
    table = local_table(height.shape[1])
    state = jnp.stack([height, east_wind, north_wind], axis=0)
    for step_index in range(STEPS):
        rates = tendency(state, cos_all, sinlat, lon_step, lat_step)
        middle = state + 0.5 * time_step * rates
        rates = tendency(middle, cos_all, sinlat, lon_step, lat_step)
        advanced = state + time_step * rates
        state = filter_state(advanced, cutoffs, table)
    return (state[0], state[1], state[2])


def solution(mesh):
    placed = (P("lat", "lon"), P("lat", "lon"), P("lat", "lon"), P())
    return jax.shard_map(
        shards,
        mesh=mesh,
        in_specs=placed,
        out_specs=(P("lat", "lon"), P("lat", "lon"), P("lat", "lon")),
        check_vma=False,
    )
```

```python
import math

import jax
import jax.numpy as jnp
from jax import lax
from jax.sharding import PartitionSpec as P

NLON = 7200
LAT_ROWS = 3600
KMAX = 64
STEPS = 2


COURANT = 0.1
OMEGA_RATE = 1.5


def local_table(width):
    waves = jnp.arange(KMAX + 1, dtype=jnp.int32)
    columns = lax.axis_index("lon") * width + jnp.arange(width, dtype=jnp.int32)
    phase = waves[:, None] * columns[None, :] % NLON
    angle = phase.astype(jnp.float32) * (2.0 * math.pi / NLON)
    return jnp.concatenate([jnp.cos(angle), jnp.sin(angle)], axis=0)


def spectral_weights(cut_rows):
    waves = jnp.arange(KMAX + 1, dtype=jnp.int32)
    scale = jnp.where(waves == 0, 1.0 / NLON, 2.0 / NLON).astype(jnp.float32)
    keep = (waves[None, :] <= cut_rows[:, None]).astype(jnp.float32) * scale[None, :]
    return jnp.concatenate([keep, keep], axis=1)


def project(fields, table):
    return jnp.einsum("fnw,kw->fnk", fields, table, precision=lax.Precision.HIGHEST)


def expand(coeffs, table):
    return jnp.einsum("fnk,kw->fnw", coeffs, table, precision=lax.Precision.HIGHEST)


def lon_sum(partial):
    devices = lax.axis_size("lon")
    fields, rows, modes = partial.shape
    share = rows // devices
    gathered = lax.all_to_all(partial, "lon", split_axis=1, concat_axis=0, tiled=True)
    reduced = gathered.reshape(devices, fields, share, modes).sum(axis=0)
    copies = jnp.broadcast_to(reduced[None], (devices, fields, share, modes))
    spread = lax.all_to_all(copies, "lon", split_axis=0, concat_axis=2, tiled=True)
    return spread.reshape(fields, rows, modes)


def low_pass(fields, cut_rows, active, table):
    weights = spectral_weights(cut_rows)
    coeffs = lon_sum(project(fields, table)) * weights[None]
    smooth = expand(coeffs, table)
    return jnp.where(active[None, :, None], smooth, fields)


def filter_state(state, cutoffs, table):
    rows_here = state.shape[1]
    lat_count = lax.axis_size("lat")
    lat_index = lax.axis_index("lat")
    filtered_rows = cutoffs.shape[0]
    cut_all = jnp.pad(cutoffs, (0, rows_here * lat_count - filtered_rows))
    global_rows = lat_index * rows_here + jnp.arange(rows_here, dtype=jnp.int32)
    cut_rows = lax.dynamic_slice_in_dim(cut_all, lat_index * rows_here, rows_here, 0)
    return low_pass(state, cut_rows, global_rows < filtered_rows, table)


def rates(ext, cos_all, sinlat, lon_step, lat_step):
    east_side = ext[:, 1:-1, 2:]
    west_side = ext[:, 1:-1, :-2]
    north_side = ext[:, :-2, 1:-1]
    south_side = ext[:, 2:, 1:-1]
    cos_north = cos_all[:-2][:, None]
    cos_south = cos_all[2:][:, None]
    coslat = cos_all[1:-1][:, None]
    sinlat = sinlat[:, None]

    def zonal_pair(east_value, west_value):
        return (east_value - west_value) * (0.5 / lon_step)

    def north_pair(north_value, south_value):
        return (north_value - south_value) * (0.5 / lat_step)

    centre = ext[:, 1:-1, 1:-1]
    height, east, north = (centre[0], centre[1], centre[2])
    inv_cos = 1.0 / coslat
    turning = 2.0 * OMEGA_RATE * sinlat + east * sinlat * inv_cos
    flux_north = north_side[0] * north_side[2] * cos_north
    flux_south = south_side[0] * south_side[2] * cos_south
    rate_height = (
        -(
            zonal_pair(east_side[0] * east_side[1], west_side[0] * west_side[1])
            + north_pair(flux_north, flux_south)
        )
        * inv_cos
    )
    rate_east = (
        -east * zonal_pair(east_side[1], west_side[1]) * inv_cos
        - north * north_pair(north_side[1], south_side[1])
        + turning * north
        - zonal_pair(east_side[0], west_side[0]) * inv_cos
    )
    rate_north = (
        -east * zonal_pair(east_side[2], west_side[2]) * inv_cos
        - north * north_pair(north_side[2], south_side[2])
        - turning * east
        - north_pair(north_side[0], south_side[0])
    )
    return jnp.stack([rate_height, rate_east, rate_north], axis=0)


def lon_shift(value, by):
    devices = lax.axis_size("lon")
    return lax.ppermute(value, "lon", [((i + by) % devices, i) for i in range(devices)])


def lat_shift(value, by):
    devices = lax.axis_size("lat")
    pairs = [(i + by, i) for i in range(devices) if 0 <= i + by < devices]
    return lax.ppermute(value, "lat", pairs)


def diagonal_shift(value, lat_by, lon_by):
    lon_count, lat_count = lax.axis_size("lon"), lax.axis_size("lat")
    pairs = []
    for lon_i in range(lon_count):
        for lat_i in range(lat_count):
            if 0 <= lat_i + lat_by < lat_count:
                source = ((lon_i + lon_by) % lon_count) * lat_count + lat_i + lat_by
                pairs.append((source, lon_i * lat_count + lat_i))
    return lax.ppermute(value, ("lon", "lat"), pairs)


def step(state, cos_two, sin_two, lon_step, lat_step, time_step):
    _, rows, width = state.shape
    lat_index = lax.axis_index("lat")
    lat_count = lax.axis_size("lat")
    half = lax.axis_size("lon") // 2
    at_pole = lat_index == 0
    at_end = lat_index == lat_count - 1
    flips = jnp.array([1.0, -1.0, -1.0], jnp.float32)

    west = lon_shift(state[:, :, width - 2:], -1)
    east = lon_shift(state[:, :, :2], 1)
    north = lat_shift(state[:, rows - 2:, :], -1)
    south = lat_shift(state[:, :2, :], 1)
    north_west = diagonal_shift(state[:, rows - 1, width - 1], -1, -1)
    north_east = diagonal_shift(state[:, rows - 1, 0], -1, 1)
    south_west = diagonal_shift(state[:, 0, width - 1], 1, -1)
    south_east = diagonal_shift(state[:, 0, 0], 1, 1)
    far_rows = lon_shift(state[:, :2, :], half)
    far_west = lon_shift(state[:, 0, width - 1], half - 1)
    far_east = lon_shift(state[:, 0, 0], half + 1)

    flip = flips[:, None]
    mirror_rows = far_rows[:, ::-1, :] * flips[:, None, None]
    north = jnp.where(at_pole, mirror_rows, north)
    north_west = jnp.where(at_pole, far_west * flips, north_west)
    north_east = jnp.where(at_pole, far_east * flips, north_east)
    last_rows = jnp.concatenate([state[:, -1:, :], state[:, -1:, :]], axis=1)
    south = jnp.where(at_end, last_rows, south)
    south_west = jnp.where(at_end, west[:, -1, 1], south_west)
    south_east = jnp.where(at_end, east[:, -1, 0], south_east)

    zero_two = jnp.zeros((3, 2, 2), jnp.float32)
    zero_one = jnp.zeros((3, 1, 1), jnp.float32)
    top_left = jnp.concatenate(
        [zero_two[:, :1], jnp.concatenate([zero_one, north_west[:, None, None]], axis=2)], axis=1
    )
    top_right = jnp.concatenate(
        [zero_two[:, :1], jnp.concatenate([north_east[:, None, None], zero_one], axis=2)], axis=1
    )
    bottom_left = jnp.concatenate(
        [jnp.concatenate([zero_one, south_west[:, None, None]], axis=2), zero_two[:, :1]], axis=1
    )
    bottom_right = jnp.concatenate(
        [jnp.concatenate([south_east[:, None, None], zero_one], axis=2), zero_two[:, :1]], axis=1
    )
    box = jnp.concatenate(
        [
            jnp.concatenate([top_left, north, top_right], axis=2),
            jnp.concatenate([west, state, east], axis=2),
            jnp.concatenate([bottom_left, south, bottom_right], axis=2),
        ],
        axis=1,
    )
    middle = box[:, 1:-1, 1:-1] + 0.5 * time_step * rates(
        box, cos_two, sin_two[1:-1], lon_step, lat_step
    )

    far_line = jnp.concatenate([far_west[:, None], far_rows[:, 0, :], far_east[:, None]], axis=1)
    near_line = jnp.pad(state[:, 0, :] * flip, ((0, 0), (1, 1)))
    next_line = jnp.pad(far_rows[:, 1, :], ((0, 0), (1, 1)))
    far_box = jnp.stack([near_line, far_line, next_line], axis=1)
    far_middle = far_rows[:, 0, :] + 0.5 * time_step * rates(
        far_box, cos_two[1:4], sin_two[2:3], lon_step, lat_step
    )[:, 0, :]
    top_middle = jnp.where(at_pole, far_middle * flip, middle[:, 0, 1:-1])
    bottom_middle = jnp.where(at_end, middle[:, -2, 1:-1], middle[:, -1, 1:-1])
    middle = jnp.concatenate(
        [
            jnp.pad(top_middle[:, None, :], ((0, 0), (0, 0), (1, 1))),
            middle[:, 1:-1, :],
            jnp.pad(bottom_middle[:, None, :], ((0, 0), (0, 0), (1, 1))),
        ],
        axis=1,
    )
    return state + time_step * rates(middle, cos_two[1:-1], sin_two[2:-2], lon_step, lat_step)


def shards(height, east_wind, north_wind, cutoffs):
    rows_here = height.shape[0]
    lat_index = lax.axis_index("lat")
    lat_step = math.pi / LAT_ROWS
    lon_step = 2.0 * math.pi / NLON
    time_step = COURANT * lat_step
    first_row = (lat_index * rows_here).astype(jnp.float32)
    index = first_row + jnp.arange(-2, rows_here + 2).astype(jnp.float32)
    cos_two = jnp.abs(jnp.sin((index + 0.5) * lat_step))
    sin_two = jnp.cos((index + 0.5) * lat_step)
    table = local_table(height.shape[1])
    state = jnp.stack([height, east_wind, north_wind], axis=0)
    for step_index in range(STEPS):
        advanced = step(state, cos_two, sin_two, lon_step, lat_step, time_step)
        state = filter_state(advanced, cutoffs, table)
    return (state[0], state[1], state[2])


def solution(mesh):
    placed = (P("lat", "lon"), P("lat", "lon"), P("lat", "lon"), P())
    return jax.shard_map(
        shards,
        mesh=mesh,
        in_specs=placed,
        out_specs=(P("lat", "lon"), P("lat", "lon"), P("lat", "lon")),
        check_vma=False,
    )
```

```python
import math

import jax
import jax.numpy as jnp
from jax import lax
from jax.sharding import PartitionSpec as P

NLON = 7200
LAT_ROWS = 3600
KMAX = 64
STEPS = 2


COURANT = 0.1
OMEGA_RATE = 1.5


def with_halo(value, sides, width, wrap):
    for axis, dim in sides:
        devices, length = (lax.axis_size(axis), value.shape[dim])
        up = [(i, (i + 1) % devices) for i in range(devices if wrap else devices - 1)]
        down = [(j, i) for i, j in up]
        last = lax.slice_in_dim(value, length - width, length, axis=dim)
        first = lax.slice_in_dim(value, 0, width, axis=dim)
        before = lax.ppermute(last, axis, up)
        after = lax.ppermute(first, axis, down)
        value = jnp.concatenate([before, value, after], axis=dim)
    return value


def from_behind(value, axis, by):
    devices = lax.axis_size(axis)
    return lax.ppermute(value, axis, [(i, (i + by) % devices) for i in range(devices)])


def local_table(first, width):
    waves = jnp.arange(KMAX + 1, dtype=jnp.int32)
    columns = (lax.axis_index("lon") * NLON // lax.axis_size("lon") + first) % NLON
    columns = (columns + jnp.arange(width, dtype=jnp.int32)) % NLON
    phase = waves[:, None] * columns[None, :] % NLON
    angle = phase.astype(jnp.float32) * (2.0 * math.pi / NLON)
    return jnp.concatenate([jnp.cos(angle), jnp.sin(angle)], axis=0)


def spectral_weights(cut_rows):
    waves = jnp.arange(KMAX + 1, dtype=jnp.int32)
    scale = jnp.where(waves == 0, 1.0 / NLON, 2.0 / NLON).astype(jnp.float32)
    keep = (waves[None, :] <= cut_rows[:, None]).astype(jnp.float32) * scale[None, :]
    return jnp.concatenate([keep, keep], axis=1)


def half_turn_signs():
    waves = jnp.arange(KMAX + 1, dtype=jnp.int32)
    signs = jnp.where(waves % 2 == 0, 1.0, -1.0).astype(jnp.float32)
    return jnp.concatenate([signs, signs], axis=0)


def project(fields, table):
    return jnp.einsum("fnw,kw->fnk", fields, table, precision=lax.Precision.HIGHEST)


def expand(coeffs, table):
    return jnp.einsum("fnk,kw->fnw", coeffs, table, precision=lax.Precision.HIGHEST)


def low_pass(fields, cut_rows, active, table, wide_table, with_halos):
    devices = lax.axis_size("lon")
    lon_index = lax.axis_index("lon")
    count, rows, width = fields.shape
    share = rows // devices
    partial = project(fields, table)
    modes = partial.shape[2]
    gathered = lax.all_to_all(partial, "lon", split_axis=1, concat_axis=0, tiled=True)
    reduced = gathered.reshape(devices, count, share, modes).sum(axis=0)
    payload = [jnp.broadcast_to(reduced.reshape(1, -1), (devices, count * share * modes))]
    if with_halos:
        targets = jnp.arange(devices, dtype=jnp.int32)[:, None]
        to_east = targets == (lon_index + 1) % devices
        edge = jnp.where(to_east, fields[:, :, -1].reshape(1, -1), fields[:, :, 0].reshape(1, -1))
        payload += [edge, jnp.broadcast_to(fields[:, 0, :].reshape(1, -1), (devices, count * width))]
    spread = lax.all_to_all(jnp.concatenate(payload, axis=1), "lon", split_axis=0, concat_axis=0, tiled=True)
    block = count * share * modes
    coeffs = spread[:, :block].reshape(devices, count, share, modes)
    coeffs = jnp.moveaxis(coeffs, 0, 1).reshape(count, rows, modes)
    weights = spectral_weights(cut_rows)
    scaled = coeffs * weights[None]
    if not with_halos:
        smooth = expand(scaled, table)
        return jnp.where(active[None, :, None], smooth, fields), None
    wide = expand(scaled, wide_table)
    smooth = wide[:, :, 1:-1]
    filtered = jnp.where(active[None, :, None], smooth, fields)
    edges = spread[:, block:block + count * rows].reshape(devices, count, rows)
    rows_far = spread[:, block + count * rows:].reshape(devices, count, width)
    west_raw = edges[(lon_index - 1) % devices]
    east_raw = edges[(lon_index + 1) % devices]
    far_raw = rows_far[(lon_index + devices // 2) % devices]
    west = jnp.where(active[None, :], wide[:, :, 0], west_raw)[:, :, None]
    east = jnp.where(active[None, :], wide[:, :, -1], east_raw)[:, :, None]
    far_smooth = expand(scaled[:, :1, :] * half_turn_signs()[None, None, :], table)[:, 0, :]
    far = jnp.where(active[0], far_smooth, far_raw)
    return filtered, (west, east, far)


def filter_state(state, cutoffs, table, wide_table, with_halos):
    rows_here = state.shape[1]
    lat_count = lax.axis_size("lat")
    lat_index = lax.axis_index("lat")
    filtered_rows = cutoffs.shape[0]
    cut_all = jnp.pad(cutoffs, (0, rows_here * lat_count - filtered_rows))
    global_rows = lat_index * rows_here + jnp.arange(rows_here, dtype=jnp.int32)
    cut_rows = lax.dynamic_slice_in_dim(cut_all, lat_index * rows_here, rows_here, 0)
    return low_pass(state, cut_rows, global_rows < filtered_rows, table, wide_table, with_halos)


def tendency(state, cos_all, sinlat, lon_step, lat_step, lon_halos=None):
    lat_index = lax.axis_index("lat")
    lat_count = lax.axis_size("lat")
    flips = jnp.array([1.0, -1.0, -1.0], jnp.float32)
    if lon_halos is None:
        edge_cols = jnp.concatenate([state[:, :, :1], state[:, :, -1:]], axis=2)
        got_cols = with_halo(edge_cols, (("lon", 2),), 1, True)
        west_col = got_cols[:, :, 0:1]
        east_col = got_cols[:, :, 3:4]
        mirror = from_behind(state[:, 0, :], "lon", lax.axis_size("lon") // 2)
    else:
        west_col, east_col, mirror = lon_halos
    mirror = mirror * flips[:, None]
    edge_rows = jnp.concatenate([state[:, :1, :], state[:, -1:, :]], axis=1)
    got_rows = with_halo(edge_rows, (("lat", 1),), 1, False)
    northmost = jnp.where(lat_index == 0, mirror, got_rows[:, 0, :])
    southmost = jnp.where(lat_index == lat_count - 1, state[:, -1, :], got_rows[:, 3, :])
    corner = jnp.zeros((3, 1, 1), jnp.float32)
    top_line = jnp.concatenate([corner, northmost[:, None, :], corner], axis=2)
    bottom_line = jnp.concatenate([corner, southmost[:, None, :], corner], axis=2)
    middle_lines = jnp.concatenate([west_col, state, east_col], axis=2)
    extended = jnp.concatenate([top_line, middle_lines, bottom_line], axis=1)
    east_side = extended[:, 1:-1, 2:]
    west_side = extended[:, 1:-1, :-2]
    north_side = extended[:, :-2, 1:-1]
    south_side = extended[:, 2:, 1:-1]
    cos_north = cos_all[:-2][:, None]
    cos_south = cos_all[2:][:, None]
    coslat = cos_all[1:-1][:, None]

    def zonal_pair(east_value, west_value):
        return (east_value - west_value) * (0.5 / lon_step)

    def north_pair(north_value, south_value):
        return (north_value - south_value) * (0.5 / lat_step)

    height, east, north = (state[0], state[1], state[2])
    inv_cos = 1.0 / coslat
    turning = 2.0 * OMEGA_RATE * sinlat + east * sinlat * inv_cos
    flux_north = north_side[0] * north_side[2] * cos_north
    flux_south = south_side[0] * south_side[2] * cos_south
    rate_height = (
        -(
            zonal_pair(east_side[0] * east_side[1], west_side[0] * west_side[1])
            + north_pair(flux_north, flux_south)
        )
        * inv_cos
    )
    rate_east = (
        -east * zonal_pair(east_side[1], west_side[1]) * inv_cos
        - north * north_pair(north_side[1], south_side[1])
        + turning * north
        - zonal_pair(east_side[0], west_side[0]) * inv_cos
    )
    rate_north = (
        -east * zonal_pair(east_side[2], west_side[2]) * inv_cos
        - north * north_pair(north_side[2], south_side[2])
        - turning * east
        - north_pair(north_side[0], south_side[0])
    )
    return jnp.stack([rate_height, rate_east, rate_north], axis=0)


def shards(height, east_wind, north_wind, cutoffs):
    rows_here = height.shape[0]
    lat_index = lax.axis_index("lat")
    lat_step = math.pi / LAT_ROWS
    lon_step = 2.0 * math.pi / NLON
    time_step = COURANT * lat_step
    first_row = (lat_index * rows_here).astype(jnp.float32)
    index = first_row + jnp.arange(-1, rows_here + 1).astype(jnp.float32)
    cos_all = jnp.abs(jnp.sin((index + 0.5) * lat_step))
    sin_all = jnp.cos((index + 0.5) * lat_step)
    sinlat = sin_all[1:-1][:, None]
    width = height.shape[1]
    table = local_table(0, width)
    wide_table = local_table(-1, width + 2)
    state = jnp.stack([height, east_wind, north_wind], axis=0)
    lon_halos = None
    for step_index in range(STEPS):
        rates = tendency(state, cos_all, sinlat, lon_step, lat_step, lon_halos)
        middle = state + 0.5 * time_step * rates
        rates = tendency(middle, cos_all, sinlat, lon_step, lat_step)
        advanced = state + time_step * rates
        last = step_index == STEPS - 1
        state, lon_halos = filter_state(advanced, cutoffs, table, wide_table, not last)
    return (state[0], state[1], state[2])


def solution(mesh):
    placed = (P("lat", "lon"), P("lat", "lon"), P("lat", "lon"), P())
    return jax.shard_map(
        shards,
        mesh=mesh,
        in_specs=placed,
        out_specs=(P("lat", "lon"), P("lat", "lon"), P("lat", "lon")),
        check_vma=False,
    )
```

```python
import math

import jax
import jax.numpy as jnp
from jax import lax
from jax.sharding import PartitionSpec as P

NLON = 7200
LAT_ROWS = 3600
KMAX = 64
STEPS = 2


COURANT = 0.1
OMEGA_RATE = 1.5


def with_halo(value, sides, width, wrap):
    for axis, dim in sides:
        devices, length = (lax.axis_size(axis), value.shape[dim])
        up = [(i, (i + 1) % devices) for i in range(devices if wrap else devices - 1)]
        down = [(j, i) for i, j in up]
        last = lax.slice_in_dim(value, length - width, length, axis=dim)
        first = lax.slice_in_dim(value, 0, width, axis=dim)
        before = lax.ppermute(last, axis, up)
        after = lax.ppermute(first, axis, down)
        value = jnp.concatenate([before, value, after], axis=dim)
    return value


def from_behind(value, axis, by):
    devices = lax.axis_size(axis)
    return lax.ppermute(value, axis, [(i, (i + by) % devices) for i in range(devices)])


def local_table(first, width):
    waves = jnp.arange(KMAX + 1, dtype=jnp.int32)
    columns = (lax.axis_index("lon") * NLON // lax.axis_size("lon") + first) % NLON
    columns = (columns + jnp.arange(width, dtype=jnp.int32)) % NLON
    phase = waves[:, None] * columns[None, :] % NLON
    angle = phase.astype(jnp.float32) * (2.0 * math.pi / NLON)
    return jnp.concatenate([jnp.cos(angle), jnp.sin(angle)], axis=0)


def spectral_weights(cut_rows):
    waves = jnp.arange(KMAX + 1, dtype=jnp.int32)
    scale = jnp.where(waves == 0, 1.0 / NLON, 2.0 / NLON).astype(jnp.float32)
    keep = (waves[None, :] <= cut_rows[:, None]).astype(jnp.float32) * scale[None, :]
    return jnp.concatenate([keep, keep], axis=1)


def half_turn_signs():
    waves = jnp.arange(KMAX + 1, dtype=jnp.int32)
    signs = jnp.where(waves % 2 == 0, 1.0, -1.0).astype(jnp.float32)
    return jnp.concatenate([signs, signs], axis=0)


def project(fields, table):
    return jnp.einsum("fnw,kw->fnk", fields, table, precision=lax.Precision.HIGHEST)


def expand(coeffs, table):
    return jnp.einsum("fnk,kw->fnw", coeffs, table, precision=lax.Precision.HIGHEST)


def low_pass(fields, cut_rows, active, table, wide_table, with_halos):
    devices = lax.axis_size("lon")
    lon_index = lax.axis_index("lon")
    count, rows, width = fields.shape
    share = rows // devices
    partial = project(fields, table)
    modes = partial.shape[2]
    gathered = lax.all_to_all(partial, "lon", split_axis=1, concat_axis=0, tiled=True)
    reduced = gathered.reshape(devices, count, share, modes).sum(axis=0)
    payload = [jnp.broadcast_to(reduced.reshape(1, -1), (devices, count * share * modes))]
    if with_halos:
        targets = jnp.arange(devices, dtype=jnp.int32)[:, None]
        to_east = targets == (lon_index + 1) % devices
        edge = jnp.where(to_east, fields[:, :, -1].reshape(1, -1), fields[:, :, 0].reshape(1, -1))
        payload += [edge, jnp.broadcast_to(fields[:, 0, :].reshape(1, -1), (devices, count * width))]
    spread = lax.all_to_all(jnp.concatenate(payload, axis=1), "lon", split_axis=0, concat_axis=0, tiled=True)
    block = count * share * modes
    coeffs = spread[:, :block].reshape(devices, count, share, modes)
    coeffs = jnp.moveaxis(coeffs, 0, 1).reshape(count, rows, modes)
    weights = spectral_weights(cut_rows)
    scaled = coeffs * weights[None]
    if not with_halos:
        smooth = expand(scaled, table)
        return jnp.where(active[None, :, None], smooth, fields), None
    wide = expand(scaled, wide_table)
    smooth = wide[:, :, 1:-1]
    filtered = jnp.where(active[None, :, None], smooth, fields)
    edges = spread[:, block:block + count * rows].reshape(devices, count, rows)
    rows_far = spread[:, block + count * rows:].reshape(devices, count, width)
    west_raw = edges[(lon_index - 1) % devices]
    east_raw = edges[(lon_index + 1) % devices]
    far_raw = rows_far[(lon_index + devices // 2) % devices]
    west = jnp.where(active[None, :], wide[:, :, 0], west_raw)[:, :, None]
    east = jnp.where(active[None, :], wide[:, :, -1], east_raw)[:, :, None]
    far_smooth = expand(scaled[:, :1, :] * half_turn_signs()[None, None, :], table)[:, 0, :]
    far = jnp.where(active[0], far_smooth, far_raw)
    return filtered, (west, east, far)


def filter_state(state, cutoffs, table, wide_table, with_halos):
    rows_here = state.shape[1]
    lat_count = lax.axis_size("lat")
    lat_index = lax.axis_index("lat")
    filtered_rows = cutoffs.shape[0]
    cut_all = jnp.pad(cutoffs, (0, rows_here * lat_count - filtered_rows))
    global_rows = lat_index * rows_here + jnp.arange(rows_here, dtype=jnp.int32)
    cut_rows = lax.dynamic_slice_in_dim(cut_all, lat_index * rows_here, rows_here, 0)
    return low_pass(state, cut_rows, global_rows < filtered_rows, table, wide_table, with_halos)


def tendency(state, cos_all, sinlat, lon_step, lat_step, lon_halos=None):
    lat_index = lax.axis_index("lat")
    lat_count = lax.axis_size("lat")
    flips = jnp.array([1.0, -1.0, -1.0], jnp.float32)
    if lon_halos is None:
        edge_cols = jnp.concatenate([state[:, :, :1], state[:, :, -1:]], axis=2)
        got_cols = with_halo(edge_cols, (("lon", 2),), 1, True)
        west_col = got_cols[:, :, 0:1]
        east_col = got_cols[:, :, 3:4]
        mirror = from_behind(state[:, 0, :], "lon", lax.axis_size("lon") // 2)
    else:
        west_col, east_col, mirror = lon_halos
    mirror = mirror * flips[:, None]
    edge_rows = jnp.concatenate([state[:, :1, :], state[:, -1:, :]], axis=1)
    got_rows = with_halo(edge_rows, (("lat", 1),), 1, False)
    northmost = jnp.where(lat_index == 0, mirror, got_rows[:, 0, :])
    southmost = jnp.where(lat_index == lat_count - 1, state[:, -1, :], got_rows[:, 3, :])
    corner = jnp.zeros((3, 1, 1), jnp.float32)
    top_line = jnp.concatenate([corner, northmost[:, None, :], corner], axis=2)
    bottom_line = jnp.concatenate([corner, southmost[:, None, :], corner], axis=2)
    middle_lines = jnp.concatenate([west_col, state, east_col], axis=2)
    extended = jnp.concatenate([top_line, middle_lines, bottom_line], axis=1)
    east_side = extended[:, 1:-1, 2:]
    west_side = extended[:, 1:-1, :-2]
    north_side = extended[:, :-2, 1:-1]
    south_side = extended[:, 2:, 1:-1]
    cos_north = cos_all[:-2][:, None]
    cos_south = cos_all[2:][:, None]
    coslat = cos_all[1:-1][:, None]

    def zonal_pair(east_value, west_value):
        return (east_value - west_value) * (0.5 / lon_step)

    def north_pair(north_value, south_value):
        return (north_value - south_value) * (0.5 / lat_step)

    height, east, north = (state[0], state[1], state[2])
    inv_cos = 1.0 / coslat
    turning = 2.0 * OMEGA_RATE * sinlat + east * sinlat * inv_cos
    flux_north = north_side[0] * north_side[2] * cos_north
    flux_south = south_side[0] * south_side[2] * cos_south
    rate_height = (
        -(
            zonal_pair(east_side[0] * east_side[1], west_side[0] * west_side[1])
            + north_pair(flux_north, flux_south)
        )
        * inv_cos
    )
    rate_east = (
        -east * zonal_pair(east_side[1], west_side[1]) * inv_cos
        - north * north_pair(north_side[1], south_side[1])
        + turning * north
        - zonal_pair(east_side[0], west_side[0]) * inv_cos
    )
    rate_north = (
        -east * zonal_pair(east_side[2], west_side[2]) * inv_cos
        - north * north_pair(north_side[2], south_side[2])
        - turning * east
        - north_pair(north_side[0], south_side[0])
    )
    return jnp.stack([rate_height, rate_east, rate_north], axis=0)


def shards(height, east_wind, north_wind, cutoffs):
    rows_here = height.shape[0]
    lat_index = lax.axis_index("lat")
    lat_step = math.pi / LAT_ROWS
    lon_step = 2.0 * math.pi / NLON
    time_step = COURANT * lat_step
    first_row = (lat_index * rows_here).astype(jnp.float32)
    index = first_row + jnp.arange(-1, rows_here + 1).astype(jnp.float32)
    cos_all = jnp.abs(jnp.sin((index + 0.5) * lat_step))
    sin_all = jnp.cos((index + 0.5) * lat_step)
    sinlat = sin_all[1:-1][:, None]
    width = height.shape[1]
    table = local_table(0, width)
    wide_table = local_table(-1, width + 2)
    state = jnp.stack([height, east_wind, north_wind], axis=0)
    edge_cols = jnp.concatenate([state[:, :, :1], state[:, :, -1:]], axis=2)
    got_cols = with_halo(edge_cols, (("lon", 2),), 1, True)
    mirror = from_behind(state[:, 0, :], "lon", lax.axis_size("lon") // 2)
    lon_halos = (got_cols[:, :, 0:1], got_cols[:, :, 3:4], mirror)

    def one_step(step_index, carry):
        state, lon_halos = carry
        rates = tendency(state, cos_all, sinlat, lon_step, lat_step, lon_halos)
        middle = state + 0.5 * time_step * rates
        rates = tendency(middle, cos_all, sinlat, lon_step, lat_step)
        advanced = state + time_step * rates
        return filter_state(advanced, cutoffs, table, wide_table, True)

    state, lon_halos = lax.fori_loop(0, STEPS, one_step, (state, lon_halos))
    return (state[0], state[1], state[2])


def solution(mesh):
    placed = (P("lat", "lon"), P("lat", "lon"), P("lat", "lon"), P())
    return jax.shard_map(
        shards,
        mesh=mesh,
        in_specs=placed,
        out_specs=(P("lat", "lon"), P("lat", "lon"), P("lat", "lon")),
        check_vma=False,
    )
```

```python
import math

import jax
import jax.numpy as jnp
from jax import lax
from jax.sharding import PartitionSpec as P

NLON = 7200
LAT_ROWS = 3600
KMAX = 64
STEPS = 2


COURANT = 0.1
OMEGA_RATE = 1.5


def with_halo(value, sides, width, wrap):
    for axis, dim in sides:
        devices, length = (lax.axis_size(axis), value.shape[dim])
        up = [(i, (i + 1) % devices) for i in range(devices if wrap else devices - 1)]
        down = [(j, i) for i, j in up]
        last = lax.slice_in_dim(value, length - width, length, axis=dim)
        first = lax.slice_in_dim(value, 0, width, axis=dim)
        before = lax.ppermute(last, axis, up)
        after = lax.ppermute(first, axis, down)
        value = jnp.concatenate([before, value, after], axis=dim)
    return value


def from_behind(value, axis, by):
    devices = lax.axis_size(axis)
    return lax.ppermute(value, axis, [(i, (i + by) % devices) for i in range(devices)])


def local_table(first, width):
    waves = jnp.arange(KMAX + 1, dtype=jnp.int32)
    columns = (lax.axis_index("lon") * NLON // lax.axis_size("lon") + first) % NLON
    columns = (columns + jnp.arange(width, dtype=jnp.int32)) % NLON
    phase = waves[:, None] * columns[None, :] % NLON
    angle = phase.astype(jnp.float32) * (2.0 * math.pi / NLON)
    return jnp.concatenate([jnp.cos(angle), jnp.sin(angle)], axis=0)


def spectral_weights(cut_rows):
    waves = jnp.arange(KMAX + 1, dtype=jnp.int32)
    scale = jnp.where(waves == 0, 1.0 / NLON, 2.0 / NLON).astype(jnp.float32)
    keep = (waves[None, :] <= cut_rows[:, None]).astype(jnp.float32) * scale[None, :]
    return jnp.concatenate([keep, keep], axis=1)


def half_turn_signs():
    waves = jnp.arange(KMAX + 1, dtype=jnp.int32)
    signs = jnp.where(waves % 2 == 0, 1.0, -1.0).astype(jnp.float32)
    return jnp.concatenate([signs, signs], axis=0)


def project(fields, table):
    return jnp.einsum("fnw,kw->fnk", fields, table, precision=lax.Precision.HIGHEST)


def expand(coeffs, table):
    return jnp.einsum("fnk,kw->fnw", coeffs, table, precision=lax.Precision.HIGHEST)


def low_pass(fields, cut_rows, active, table, wide_table, with_halos):
    devices = lax.axis_size("lon")
    lon_index = lax.axis_index("lon")
    count, rows, width = fields.shape
    share = rows // devices
    partial = project(fields, table)
    modes = partial.shape[2]
    gathered = lax.all_to_all(partial, "lon", split_axis=1, concat_axis=0, tiled=True)
    reduced = gathered.reshape(devices, count, share, modes).sum(axis=0)
    payload = [jnp.broadcast_to(reduced.reshape(1, -1), (devices, count * share * modes))]
    if with_halos:
        targets = jnp.arange(devices, dtype=jnp.int32)[:, None]
        to_east = targets == (lon_index + 1) % devices
        edge = jnp.where(to_east, fields[:, :, -1].reshape(1, -1), fields[:, :, 0].reshape(1, -1))
        payload += [edge, jnp.broadcast_to(fields[:, 0, :].reshape(1, -1), (devices, count * width))]
    spread = lax.all_to_all(jnp.concatenate(payload, axis=1), "lon", split_axis=0, concat_axis=0, tiled=True)
    block = count * share * modes
    coeffs = spread[:, :block].reshape(devices, count, share, modes)
    coeffs = jnp.moveaxis(coeffs, 0, 1).reshape(count, rows, modes)
    weights = spectral_weights(cut_rows)
    scaled = coeffs * weights[None]
    if not with_halos:
        smooth = expand(scaled, table)
        return jnp.where(active[None, :, None], smooth, fields), None, None
    wide = expand(scaled, wide_table)
    smooth = wide[:, :, 1:-1]
    filtered = jnp.where(active[None, :, None], smooth, fields)
    edges = spread[:, block:block + count * rows].reshape(devices, count, rows)
    rows_far = spread[:, block + count * rows:].reshape(devices, count, width)
    west_raw = edges[(lon_index - 1) % devices]
    east_raw = edges[(lon_index + 1) % devices]
    far_raw = rows_far[(lon_index + devices // 2) % devices]
    west = jnp.where(active[None, :], wide[:, :, 0], west_raw)[:, :, None]
    east = jnp.where(active[None, :], wide[:, :, -1], east_raw)[:, :, None]
    far_wide = expand(scaled[:, :2, :] * half_turn_signs()[None, None, :], wide_table)
    far = jnp.where(active[0], far_wide[:, 0, 1:-1], far_raw)
    return filtered, (west, east, far), (far_wide, wide[:, 0, :])


def filter_state(state, cutoffs, table, wide_table, with_halos):
    rows_here = state.shape[1]
    lat_count = lax.axis_size("lat")
    lat_index = lax.axis_index("lat")
    filtered_rows = cutoffs.shape[0]
    cut_all = jnp.pad(cutoffs, (0, rows_here * lat_count - filtered_rows))
    global_rows = lat_index * rows_here + jnp.arange(rows_here, dtype=jnp.int32)
    cut_rows = lax.dynamic_slice_in_dim(cut_all, lat_index * rows_here, rows_here, 0)
    return low_pass(state, cut_rows, global_rows < filtered_rows, table, wide_table, with_halos)


def rates(ext, cos_all, sinlat, lon_step, lat_step):
    east_side = ext[:, 1:-1, 2:]
    west_side = ext[:, 1:-1, :-2]
    north_side = ext[:, :-2, 1:-1]
    south_side = ext[:, 2:, 1:-1]
    cos_north = cos_all[:-2][:, None]
    cos_south = cos_all[2:][:, None]
    coslat = cos_all[1:-1][:, None]
    sinlat = sinlat[:, None]

    def zonal_pair(east_value, west_value):
        return (east_value - west_value) * (0.5 / lon_step)

    def north_pair(north_value, south_value):
        return (north_value - south_value) * (0.5 / lat_step)

    centre = ext[:, 1:-1, 1:-1]
    height, east, north = (centre[0], centre[1], centre[2])
    inv_cos = 1.0 / coslat
    turning = 2.0 * OMEGA_RATE * sinlat + east * sinlat * inv_cos
    flux_north = north_side[0] * north_side[2] * cos_north
    flux_south = south_side[0] * south_side[2] * cos_south
    rate_height = (
        -(
            zonal_pair(east_side[0] * east_side[1], west_side[0] * west_side[1])
            + north_pair(flux_north, flux_south)
        )
        * inv_cos
    )
    rate_east = (
        -east * zonal_pair(east_side[1], west_side[1]) * inv_cos
        - north * north_pair(north_side[1], south_side[1])
        + turning * north
        - zonal_pair(east_side[0], west_side[0]) * inv_cos
    )
    rate_north = (
        -east * zonal_pair(east_side[2], west_side[2]) * inv_cos
        - north * north_pair(north_side[2], south_side[2])
        - turning * east
        - north_pair(north_side[0], south_side[0])
    )
    return jnp.stack([rate_height, rate_east, rate_north], axis=0)


def tendency(state, cos_all, sinlat, lon_step, lat_step, lon_halos=None, far=None):
    lat_index = lax.axis_index("lat")
    lat_count = lax.axis_size("lat")
    flips = jnp.array([1.0, -1.0, -1.0], jnp.float32)
    if lon_halos is None:
        edge_cols = jnp.concatenate([state[:, :, :1], state[:, :, -1:]], axis=2)
        got_cols = with_halo(edge_cols, (("lon", 2),), 1, True)
        west_col = got_cols[:, :, 0:1]
        east_col = got_cols[:, :, 3:4]
        if far is None:
            mirror = from_behind(state[:, 0, :], "lon", lax.axis_size("lon") // 2)
        else:
            mirror = far
    else:
        west_col, east_col, mirror = lon_halos
    mirror = mirror * flips[:, None]
    edge_rows = jnp.concatenate([state[:, :1, :], state[:, -1:, :]], axis=1)
    got_rows = with_halo(edge_rows, (("lat", 1),), 1, False)
    northmost = jnp.where(lat_index == 0, mirror, got_rows[:, 0, :])
    southmost = jnp.where(lat_index == lat_count - 1, state[:, -1, :], got_rows[:, 3, :])
    corner = jnp.zeros((3, 1, 1), jnp.float32)
    top_line = jnp.concatenate([corner, northmost[:, None, :], corner], axis=2)
    bottom_line = jnp.concatenate([corner, southmost[:, None, :], corner], axis=2)
    middle_lines = jnp.concatenate([west_col, state, east_col], axis=2)
    extended = jnp.concatenate([top_line, middle_lines, bottom_line], axis=1)
    east_side = extended[:, 1:-1, 2:]
    west_side = extended[:, 1:-1, :-2]
    north_side = extended[:, :-2, 1:-1]
    south_side = extended[:, 2:, 1:-1]
    cos_north = cos_all[:-2][:, None]
    cos_south = cos_all[2:][:, None]
    coslat = cos_all[1:-1][:, None]

    def zonal_pair(east_value, west_value):
        return (east_value - west_value) * (0.5 / lon_step)

    def north_pair(north_value, south_value):
        return (north_value - south_value) * (0.5 / lat_step)

    height, east, north = (state[0], state[1], state[2])
    inv_cos = 1.0 / coslat
    turning = 2.0 * OMEGA_RATE * sinlat + east * sinlat * inv_cos
    flux_north = north_side[0] * north_side[2] * cos_north
    flux_south = south_side[0] * south_side[2] * cos_south
    rate_height = (
        -(
            zonal_pair(east_side[0] * east_side[1], west_side[0] * west_side[1])
            + north_pair(flux_north, flux_south)
        )
        * inv_cos
    )
    rate_east = (
        -east * zonal_pair(east_side[1], west_side[1]) * inv_cos
        - north * north_pair(north_side[1], south_side[1])
        + turning * north
        - zonal_pair(east_side[0], west_side[0]) * inv_cos
    )
    rate_north = (
        -east * zonal_pair(east_side[2], west_side[2]) * inv_cos
        - north * north_pair(north_side[2], south_side[2])
        - turning * east
        - north_pair(north_side[0], south_side[0])
    )
    return jnp.stack([rate_height, rate_east, rate_north], axis=0)


def shards(height, east_wind, north_wind, cutoffs):
    rows_here = height.shape[0]
    lat_index = lax.axis_index("lat")
    lat_step = math.pi / LAT_ROWS
    lon_step = 2.0 * math.pi / NLON
    time_step = COURANT * lat_step
    first_row = (lat_index * rows_here).astype(jnp.float32)
    index = first_row + jnp.arange(-1, rows_here + 1).astype(jnp.float32)
    cos_all = jnp.abs(jnp.sin((index + 0.5) * lat_step))
    sin_all = jnp.cos((index + 0.5) * lat_step)
    sinlat = sin_all[1:-1][:, None]
    width = height.shape[1]
    table = local_table(0, width)
    wide_table = local_table(-1, width + 2)
    state = jnp.stack([height, east_wind, north_wind], axis=0)
    lon_halos = None
    pole = None
    flips = jnp.array([1.0, -1.0, -1.0], jnp.float32)[:, None]
    for step_index in range(STEPS):
        rates_now = tendency(state, cos_all, sinlat, lon_step, lat_step, lon_halos)
        middle = state + 0.5 * time_step * rates_now
        far = None
        if pole is not None:
            far_wide, near_row = pole
            far_box = jnp.stack([near_row * flips, far_wide[:, 0, :], far_wide[:, 1, :]], axis=1)
            far_rate = rates(far_box, cos_all[0:3], sin_all[1:2], lon_step, lat_step)[:, 0, :]
            far = far_wide[:, 0, 1:-1] + 0.5 * time_step * far_rate
        rates_now = tendency(middle, cos_all, sinlat, lon_step, lat_step, None, far)
        advanced = state + time_step * rates_now
        last = step_index == STEPS - 1
        state, lon_halos, pole = filter_state(advanced, cutoffs, table, wide_table, not last)
    return (state[0], state[1], state[2])


def solution(mesh):
    placed = (P("lat", "lon"), P("lat", "lon"), P("lat", "lon"), P())
    return jax.shard_map(
        shards,
        mesh=mesh,
        in_specs=placed,
        out_specs=(P("lat", "lon"), P("lat", "lon"), P("lat", "lon")),
        check_vma=False,
    )
```

```python
import math

import jax
import jax.numpy as jnp
from jax import lax
from jax.sharding import PartitionSpec as P

NLON = 7200
LAT_ROWS = 3600
KMAX = 64
STEPS = 2


COURANT = 0.1
OMEGA_RATE = 1.5


def with_halo(value, sides, width, wrap):
    for axis, dim in sides:
        devices, length = (lax.axis_size(axis), value.shape[dim])
        up = [(i, (i + 1) % devices) for i in range(devices if wrap else devices - 1)]
        down = [(j, i) for i, j in up]
        last = lax.slice_in_dim(value, length - width, length, axis=dim)
        first = lax.slice_in_dim(value, 0, width, axis=dim)
        before = lax.ppermute(last, axis, up)
        after = lax.ppermute(first, axis, down)
        value = jnp.concatenate([before, value, after], axis=dim)
    return value


def from_behind(value, axis, by):
    devices = lax.axis_size(axis)
    return lax.ppermute(value, axis, [(i, (i + by) % devices) for i in range(devices)])


def lat_shift(value, by):
    devices = lax.axis_size("lat")
    pairs = [(i + by, i) for i in range(devices) if 0 <= i + by < devices]
    return lax.ppermute(value, "lat", pairs)


def local_table(first, width):
    waves = jnp.arange(KMAX + 1, dtype=jnp.int32)
    columns = (lax.axis_index("lon") * NLON // lax.axis_size("lon") + first) % NLON
    columns = (columns + jnp.arange(width, dtype=jnp.int32)) % NLON
    phase = waves[:, None] * columns[None, :] % NLON
    angle = phase.astype(jnp.float32) * (2.0 * math.pi / NLON)
    return jnp.concatenate([jnp.cos(angle), jnp.sin(angle)], axis=0)


def spectral_weights(cut_rows):
    waves = jnp.arange(KMAX + 1, dtype=jnp.int32)
    scale = jnp.where(waves == 0, 1.0 / NLON, 2.0 / NLON).astype(jnp.float32)
    keep = (waves[None, :] <= cut_rows[:, None]).astype(jnp.float32) * scale[None, :]
    return jnp.concatenate([keep, keep], axis=1)


def half_turn_signs():
    waves = jnp.arange(KMAX + 1, dtype=jnp.int32)
    signs = jnp.where(waves % 2 == 0, 1.0, -1.0).astype(jnp.float32)
    return jnp.concatenate([signs, signs], axis=0)


def project(fields, table):
    return jnp.einsum("fnw,kw->fnk", fields, table, precision=lax.Precision.HIGHEST)


def expand(coeffs, table):
    return jnp.einsum("fnk,kw->fnw", coeffs, table, precision=lax.Precision.HIGHEST)


def low_pass(fields, cut_rows, active, table, wide_table, with_halos):
    devices = lax.axis_size("lon")
    lon_index = lax.axis_index("lon")
    count, rows, width = fields.shape
    share = rows // devices
    partial = project(fields, table)
    modes = partial.shape[2]
    gathered = lax.all_to_all(partial, "lon", split_axis=1, concat_axis=0, tiled=True)
    reduced = gathered.reshape(devices, count, share, modes).sum(axis=0)
    payload = [jnp.broadcast_to(reduced.reshape(1, -1), (devices, count * share * modes))]
    if with_halos:
        targets = jnp.arange(devices, dtype=jnp.int32)[:, None]
        to_east = targets == (lon_index + 1) % devices
        last_two = fields[:, :, width - 2:].reshape(1, -1)
        first_two = fields[:, :, :2].reshape(1, -1)
        payload += [jnp.where(to_east, last_two, first_two)]
    spread = lax.all_to_all(jnp.concatenate(payload, axis=1), "lon", split_axis=0, concat_axis=0, tiled=True)
    block = count * share * modes
    coeffs = spread[:, :block].reshape(devices, count, share, modes)
    coeffs = jnp.moveaxis(coeffs, 0, 1).reshape(count, rows, modes)
    weights = spectral_weights(cut_rows)
    scaled = coeffs * weights[None]
    if not with_halos:
        smooth = expand(scaled, table)
        return jnp.where(active[None, :, None], smooth, fields), None
    wide = expand(scaled, wide_table)
    filtered = jnp.where(active[None, :, None], wide[:, :, 2:-2], fields)
    edges = spread[:, block:].reshape(devices, count, rows, 2)
    west = jnp.where(active[None, :, None], wide[:, :, :2], edges[(lon_index - 1) % devices])
    east = jnp.where(active[None, :, None], wide[:, :, -2:], edges[(lon_index + 1) % devices])
    far_wide = expand(scaled[:, :2, :] * half_turn_signs()[None, None, :], wide_table)[:, :, 1:-1]
    return filtered, (west, east, far_wide, wide[:, 0, 1:-1])


def filter_state(state, cutoffs, table, wide_table, with_halos):
    rows_here = state.shape[1]
    lat_count = lax.axis_size("lat")
    lat_index = lax.axis_index("lat")
    filtered_rows = cutoffs.shape[0]
    cut_all = jnp.pad(cutoffs, (0, rows_here * lat_count - filtered_rows))
    global_rows = lat_index * rows_here + jnp.arange(rows_here, dtype=jnp.int32)
    cut_rows = lax.dynamic_slice_in_dim(cut_all, lat_index * rows_here, rows_here, 0)
    return low_pass(state, cut_rows, global_rows < filtered_rows, table, wide_table, with_halos)


def rates(ext, cos_all, sinlat, lon_step, lat_step):
    east_side = ext[:, 1:-1, 2:]
    west_side = ext[:, 1:-1, :-2]
    north_side = ext[:, :-2, 1:-1]
    south_side = ext[:, 2:, 1:-1]
    cos_north = cos_all[:-2][:, None]
    cos_south = cos_all[2:][:, None]
    coslat = cos_all[1:-1][:, None]
    sinlat = sinlat[:, None]

    def zonal_pair(east_value, west_value):
        return (east_value - west_value) * (0.5 / lon_step)

    def north_pair(north_value, south_value):
        return (north_value - south_value) * (0.5 / lat_step)

    centre = ext[:, 1:-1, 1:-1]
    height, east, north = (centre[0], centre[1], centre[2])
    inv_cos = 1.0 / coslat
    turning = 2.0 * OMEGA_RATE * sinlat + east * sinlat * inv_cos
    flux_north = north_side[0] * north_side[2] * cos_north
    flux_south = south_side[0] * south_side[2] * cos_south
    rate_height = (
        -(
            zonal_pair(east_side[0] * east_side[1], west_side[0] * west_side[1])
            + north_pair(flux_north, flux_south)
        )
        * inv_cos
    )
    rate_east = (
        -east * zonal_pair(east_side[1], west_side[1]) * inv_cos
        - north * north_pair(north_side[1], south_side[1])
        + turning * north
        - zonal_pair(east_side[0], west_side[0]) * inv_cos
    )
    rate_north = (
        -east * zonal_pair(east_side[2], west_side[2]) * inv_cos
        - north * north_pair(north_side[2], south_side[2])
        - turning * east
        - north_pair(north_side[0], south_side[0])
    )
    return jnp.stack([rate_height, rate_east, rate_north], axis=0)


def tendency(state, cos_all, sinlat, lon_step, lat_step, lon_halos=None, far=None):
    lat_index = lax.axis_index("lat")
    lat_count = lax.axis_size("lat")
    flips = jnp.array([1.0, -1.0, -1.0], jnp.float32)
    if lon_halos is None:
        edge_cols = jnp.concatenate([state[:, :, :1], state[:, :, -1:]], axis=2)
        got_cols = with_halo(edge_cols, (("lon", 2),), 1, True)
        west_col = got_cols[:, :, 0:1]
        east_col = got_cols[:, :, 3:4]
        if far is None:
            mirror = from_behind(state[:, 0, :], "lon", lax.axis_size("lon") // 2)
        else:
            mirror = far
    else:
        west_col, east_col, mirror = lon_halos
    mirror = mirror * flips[:, None]
    edge_rows = jnp.concatenate([state[:, :1, :], state[:, -1:, :]], axis=1)
    got_rows = with_halo(edge_rows, (("lat", 1),), 1, False)
    northmost = jnp.where(lat_index == 0, mirror, got_rows[:, 0, :])
    southmost = jnp.where(lat_index == lat_count - 1, state[:, -1, :], got_rows[:, 3, :])
    return stencil(state, west_col, east_col, northmost, southmost, cos_all, sinlat, lon_step, lat_step)


def stencil(state, west_col, east_col, northmost, southmost, cos_all, sinlat, lon_step, lat_step):
    corner = jnp.zeros((3, 1, 1), jnp.float32)
    top_line = jnp.concatenate([corner, northmost[:, None, :], corner], axis=2)
    bottom_line = jnp.concatenate([corner, southmost[:, None, :], corner], axis=2)
    middle_lines = jnp.concatenate([west_col, state, east_col], axis=2)
    extended = jnp.concatenate([top_line, middle_lines, bottom_line], axis=1)
    east_side = extended[:, 1:-1, 2:]
    west_side = extended[:, 1:-1, :-2]
    north_side = extended[:, :-2, 1:-1]
    south_side = extended[:, 2:, 1:-1]
    cos_north = cos_all[:-2][:, None]
    cos_south = cos_all[2:][:, None]
    coslat = cos_all[1:-1][:, None]

    def zonal_pair(east_value, west_value):
        return (east_value - west_value) * (0.5 / lon_step)

    def north_pair(north_value, south_value):
        return (north_value - south_value) * (0.5 / lat_step)

    height, east, north = (state[0], state[1], state[2])
    inv_cos = 1.0 / coslat
    turning = 2.0 * OMEGA_RATE * sinlat + east * sinlat * inv_cos
    flux_north = north_side[0] * north_side[2] * cos_north
    flux_south = south_side[0] * south_side[2] * cos_south
    rate_height = (
        -(
            zonal_pair(east_side[0] * east_side[1], west_side[0] * west_side[1])
            + north_pair(flux_north, flux_south)
        )
        * inv_cos
    )
    rate_east = (
        -east * zonal_pair(east_side[1], west_side[1]) * inv_cos
        - north * north_pair(north_side[1], south_side[1])
        + turning * north
        - zonal_pair(east_side[0], west_side[0]) * inv_cos
    )
    rate_north = (
        -east * zonal_pair(east_side[2], west_side[2]) * inv_cos
        - north * north_pair(north_side[2], south_side[2])
        - turning * east
        - north_pair(north_side[0], south_side[0])
    )
    return jnp.stack([rate_height, rate_east, rate_north], axis=0)


def second_step(state, halos, cos_two, sin_two, lon_step, lat_step, time_step):
    west_two, east_two, far_wide, near_row = halos
    _, rows, width = state.shape
    lat_index = lax.axis_index("lat")
    at_pole = lat_index == 0
    at_end = lat_index == lax.axis_size("lat") - 1
    flip = jnp.array([1.0, -1.0, -1.0], jnp.float32)[:, None]
    cos_all = cos_two[1:-1]
    sinlat = sin_two[2:-2][:, None]

    wide_rows = jnp.concatenate([west_two[:, :, 1:], state, east_two[:, :, :1]], axis=2)
    north_rows = lat_shift(wide_rows[:, rows - 2:, :], -1)
    south_rows = lat_shift(wide_rows[:, :2, :], 1)
    pole_rows = jnp.stack([far_wide[:, 1, :], far_wide[:, 0, :]], axis=1) * flip[:, :, None]
    north_rows = jnp.where(at_pole, pole_rows, north_rows)
    end_rows = jnp.concatenate([wide_rows[:, -1:, :], wide_rows[:, -1:, :]], axis=1)
    south_rows = jnp.where(at_end, end_rows, south_rows)

    rates_now = stencil(
        state, west_two[:, :, 1:], east_two[:, :, :1], north_rows[:, 1, 1:-1], south_rows[:, 0, 1:-1],
        cos_all, sinlat, lon_step, lat_step,
    )
    middle = state + 0.5 * time_step * rates_now

    zero = jnp.zeros((3, 1, 1), jnp.float32)
    west_box = jnp.concatenate(
        [
            jnp.concatenate([zero, north_rows[:, 1:2, 0:2]], axis=2),
            jnp.concatenate([west_two, state[:, :, :1]], axis=2),
            jnp.concatenate([zero, south_rows[:, 0:1, 0:2]], axis=2),
        ],
        axis=1,
    )
    east_box = jnp.concatenate(
        [
            jnp.concatenate([north_rows[:, 1:2, width:], zero], axis=2),
            jnp.concatenate([state[:, :, width - 1:], east_two], axis=2),
            jnp.concatenate([south_rows[:, 0:1, width:], zero], axis=2),
        ],
        axis=1,
    )
    west_mid = west_two[:, :, 1:] + 0.5 * time_step * rates(west_box, cos_all, sin_two[2:-2], lon_step, lat_step)
    east_mid = east_two[:, :, :1] + 0.5 * time_step * rates(east_box, cos_all, sin_two[2:-2], lon_step, lat_step)
    north_box = jnp.concatenate([north_rows, wide_rows[:, :1, :]], axis=1)
    north_mid = north_rows[:, 1, 1:-1] + 0.5 * time_step * rates(
        north_box, cos_two[0:3], sin_two[1:2], lon_step, lat_step
    )[:, 0, :]
    south_box = jnp.concatenate([wide_rows[:, -1:, :], south_rows], axis=1)
    south_mid = south_rows[:, 0, 1:-1] + 0.5 * time_step * rates(
        south_box, cos_two[rows + 1:rows + 4], sin_two[rows + 2:rows + 3], lon_step, lat_step
    )[:, 0, :]
    far_box = jnp.stack([near_row * flip, far_wide[:, 0, :], far_wide[:, 1, :]], axis=1)
    far_mid = far_wide[:, 0, 1:-1] + 0.5 * time_step * rates(
        far_box, cos_two[1:4], sin_two[2:3], lon_step, lat_step
    )[:, 0, :]
    north_mid = jnp.where(at_pole, far_mid * flip, north_mid)
    south_mid = jnp.where(at_end, middle[:, -1, :], south_mid)
    rates_now = stencil(
        middle, west_mid, east_mid, north_mid, south_mid, cos_all, sinlat, lon_step, lat_step
    )
    return state + time_step * rates_now


def shards(height, east_wind, north_wind, cutoffs):
    rows_here = height.shape[0]
    lat_index = lax.axis_index("lat")
    lat_step = math.pi / LAT_ROWS
    lon_step = 2.0 * math.pi / NLON
    time_step = COURANT * lat_step
    first_row = (lat_index * rows_here).astype(jnp.float32)
    index = first_row + jnp.arange(-2, rows_here + 2).astype(jnp.float32)
    cos_two = jnp.abs(jnp.sin((index + 0.5) * lat_step))
    sin_two = jnp.cos((index + 0.5) * lat_step)
    cos_all = cos_two[1:-1]
    sinlat = sin_two[2:-2][:, None]
    width = height.shape[1]
    table = local_table(0, width)
    wide_table = local_table(-2, width + 4)
    state = jnp.stack([height, east_wind, north_wind], axis=0)
    for step_index in range(STEPS):
        last = step_index == STEPS - 1
        if step_index == 0:
            rates_now = tendency(state, cos_all, sinlat, lon_step, lat_step)
            middle = state + 0.5 * time_step * rates_now
            rates_now = tendency(middle, cos_all, sinlat, lon_step, lat_step)
            advanced = state + time_step * rates_now
        else:
            advanced = second_step(state, halos, cos_two, sin_two, lon_step, lat_step, time_step)
        state, halos = filter_state(advanced, cutoffs, table, wide_table, not last)
    return (state[0], state[1], state[2])


def solution(mesh):
    placed = (P("lat", "lon"), P("lat", "lon"), P("lat", "lon"), P())
    return jax.shard_map(
        shards,
        mesh=mesh,
        in_specs=placed,
        out_specs=(P("lat", "lon"), P("lat", "lon"), P("lat", "lon")),
        check_vma=False,
    )
```

```python
import math

import jax
import jax.numpy as jnp
from jax import lax
from jax.sharding import PartitionSpec as P

NLON = 7200
LAT_ROWS = 3600
KMAX = 64
STEPS = 2


COURANT = 0.1
OMEGA_RATE = 1.5


def with_halo(value, sides, width, wrap):
    for axis, dim in sides:
        devices, length = (lax.axis_size(axis), value.shape[dim])
        up = [(i, (i + 1) % devices) for i in range(devices if wrap else devices - 1)]
        down = [(j, i) for i, j in up]
        last = lax.slice_in_dim(value, length - width, length, axis=dim)
        first = lax.slice_in_dim(value, 0, width, axis=dim)
        before = lax.ppermute(last, axis, up)
        after = lax.ppermute(first, axis, down)
        value = jnp.concatenate([before, value, after], axis=dim)
    return value


def from_behind(value, axis, by):
    devices = lax.axis_size(axis)
    return lax.ppermute(value, axis, [(i, (i + by) % devices) for i in range(devices)])


def lat_shift(value, by):
    devices = lax.axis_size("lat")
    pairs = [(i + by, i) for i in range(devices) if 0 <= i + by < devices]
    return lax.ppermute(value, "lat", pairs)


def local_table(first, width):
    waves = jnp.arange(KMAX + 1, dtype=jnp.int32)
    columns = (lax.axis_index("lon") * NLON // lax.axis_size("lon") + first) % NLON
    columns = (columns + jnp.arange(width, dtype=jnp.int32)) % NLON
    phase = waves[:, None] * columns[None, :] % NLON
    angle = phase.astype(jnp.float32) * (2.0 * math.pi / NLON)
    return jnp.concatenate([jnp.cos(angle), jnp.sin(angle)], axis=0)


def spectral_weights(cut_rows):
    waves = jnp.arange(KMAX + 1, dtype=jnp.int32)
    scale = jnp.where(waves == 0, 1.0 / NLON, 2.0 / NLON).astype(jnp.float32)
    keep = (waves[None, :] <= cut_rows[:, None]).astype(jnp.float32) * scale[None, :]
    return jnp.concatenate([keep, keep], axis=1)


def half_turn_signs():
    waves = jnp.arange(KMAX + 1, dtype=jnp.int32)
    signs = jnp.where(waves % 2 == 0, 1.0, -1.0).astype(jnp.float32)
    return jnp.concatenate([signs, signs], axis=0)


def project(fields, table):
    return jnp.einsum("fnw,kw->fnk", fields, table, precision=lax.Precision.HIGHEST)


def expand(coeffs, table):
    return jnp.einsum("fnk,kw->fnw", coeffs, table, precision=lax.Precision.HIGHEST)


def low_pass(fields, cut_rows, active, table, wide_table, with_halos):
    devices = lax.axis_size("lon")
    lon_index = lax.axis_index("lon")
    count, rows, width = fields.shape
    share = rows // devices
    partial = project(fields, table)
    modes = partial.shape[2]
    gathered = lax.all_to_all(partial, "lon", split_axis=1, concat_axis=0, tiled=True)
    reduced = gathered.reshape(devices, count, share, modes).sum(axis=0)
    payload = [jnp.broadcast_to(reduced.reshape(1, -1), (devices, count * share * modes))]
    if with_halos:
        targets = jnp.arange(devices, dtype=jnp.int32)[:, None]
        to_east = targets == (lon_index + 1) % devices
        last_two = fields[:, :, width - 2:].reshape(1, -1)
        first_two = fields[:, :, :2].reshape(1, -1)
        payload += [jnp.where(to_east, last_two, first_two)]
    spread = lax.all_to_all(jnp.concatenate(payload, axis=1), "lon", split_axis=0, concat_axis=0, tiled=True)
    block = count * share * modes
    coeffs = spread[:, :block].reshape(devices, count, share, modes)
    coeffs = jnp.moveaxis(coeffs, 0, 1).reshape(count, rows, modes)
    weights = spectral_weights(cut_rows)
    scaled = coeffs * weights[None]
    if not with_halos:
        smooth = expand(scaled, table)
        return jnp.where(active[None, :, None], smooth, fields), None
    wide = expand(scaled, wide_table)
    filtered = jnp.where(active[None, :, None], wide[:, :, 2:-2], fields)
    edges = spread[:, block:].reshape(devices, count, rows, 2)
    west = jnp.where(active[None, :, None], wide[:, :, :2], edges[(lon_index - 1) % devices])
    east = jnp.where(active[None, :, None], wide[:, :, -2:], edges[(lon_index + 1) % devices])
    far_wide = expand(scaled[:, :2, :] * half_turn_signs()[None, None, :], wide_table)[:, :, 1:-1]
    return filtered, (west, east, far_wide, wide[:, 0, 1:-1])


def filter_state(state, cutoffs, table, wide_table, with_halos):
    rows_here = state.shape[1]
    lat_count = lax.axis_size("lat")
    lat_index = lax.axis_index("lat")
    filtered_rows = cutoffs.shape[0]
    cut_all = jnp.pad(cutoffs, (0, rows_here * lat_count - filtered_rows))
    global_rows = lat_index * rows_here + jnp.arange(rows_here, dtype=jnp.int32)
    cut_rows = lax.dynamic_slice_in_dim(cut_all, lat_index * rows_here, rows_here, 0)
    return low_pass(state, cut_rows, global_rows < filtered_rows, table, wide_table, with_halos)


def tendency(state, cos_all, sinlat, lon_step, lat_step, lon_halos=None, far=None):
    lat_index = lax.axis_index("lat")
    lat_count = lax.axis_size("lat")
    flips = jnp.array([1.0, -1.0, -1.0], jnp.float32)
    if lon_halos is None:
        edge_cols = jnp.concatenate([state[:, :, :1], state[:, :, -1:]], axis=2)
        got_cols = with_halo(edge_cols, (("lon", 2),), 1, True)
        west_col = got_cols[:, :, 0:1]
        east_col = got_cols[:, :, 3:4]
        if far is None:
            mirror = from_behind(state[:, 0, :], "lon", lax.axis_size("lon") // 2)
        else:
            mirror = far
    else:
        west_col, east_col, mirror = lon_halos
    mirror = mirror * flips[:, None]
    edge_rows = jnp.concatenate([state[:, :1, :], state[:, -1:, :]], axis=1)
    got_rows = with_halo(edge_rows, (("lat", 1),), 1, False)
    northmost = jnp.where(lat_index == 0, mirror, got_rows[:, 0, :])
    southmost = jnp.where(lat_index == lat_count - 1, state[:, -1, :], got_rows[:, 3, :])
    return stencil(state, west_col, east_col, northmost, southmost, cos_all, sinlat, lon_step, lat_step)


def stencil(state, west_col, east_col, northmost, southmost, cos_all, sinlat, lon_step, lat_step):
    corner = jnp.zeros((3, 1, 1), jnp.float32)
    top_line = jnp.concatenate([corner, northmost[:, None, :], corner], axis=2)
    bottom_line = jnp.concatenate([corner, southmost[:, None, :], corner], axis=2)
    middle_lines = jnp.concatenate([west_col, state, east_col], axis=2)
    extended = jnp.concatenate([top_line, middle_lines, bottom_line], axis=1)
    east_side = extended[:, 1:-1, 2:]
    west_side = extended[:, 1:-1, :-2]
    north_side = extended[:, :-2, 1:-1]
    south_side = extended[:, 2:, 1:-1]
    cos_north = cos_all[:-2][:, None]
    cos_south = cos_all[2:][:, None]
    coslat = cos_all[1:-1][:, None]

    def zonal_pair(east_value, west_value):
        return (east_value - west_value) * (0.5 / lon_step)

    def north_pair(north_value, south_value):
        return (north_value - south_value) * (0.5 / lat_step)

    height, east, north = (state[0], state[1], state[2])
    inv_cos = 1.0 / coslat
    turning = 2.0 * OMEGA_RATE * sinlat + east * sinlat * inv_cos
    flux_north = north_side[0] * north_side[2] * cos_north
    flux_south = south_side[0] * south_side[2] * cos_south
    rate_height = (
        -(
            zonal_pair(east_side[0] * east_side[1], west_side[0] * west_side[1])
            + north_pair(flux_north, flux_south)
        )
        * inv_cos
    )
    rate_east = (
        -east * zonal_pair(east_side[1], west_side[1]) * inv_cos
        - north * north_pair(north_side[1], south_side[1])
        + turning * north
        - zonal_pair(east_side[0], west_side[0]) * inv_cos
    )
    rate_north = (
        -east * zonal_pair(east_side[2], west_side[2]) * inv_cos
        - north * north_pair(north_side[2], south_side[2])
        - turning * east
        - north_pair(north_side[0], south_side[0])
    )
    return jnp.stack([rate_height, rate_east, rate_north], axis=0)


def point_rates(centre, east, west, north, south, cos_north, cos_south, coslat, sinlat, lon_step, lat_step):
    def zonal_pair(east_value, west_value):
        return (east_value - west_value) * (0.5 / lon_step)

    def north_pair(north_value, south_value):
        return (north_value - south_value) * (0.5 / lat_step)

    height, east_wind, north_wind = (centre[0], centre[1], centre[2])
    inv_cos = 1.0 / coslat
    turning = 2.0 * OMEGA_RATE * sinlat + east_wind * sinlat * inv_cos
    flux_north = north[0] * north[2] * cos_north
    flux_south = south[0] * south[2] * cos_south
    rate_height = -(zonal_pair(east[0] * east[1], west[0] * west[1]) + north_pair(flux_north, flux_south)) * inv_cos
    rate_east = (
        -east_wind * zonal_pair(east[1], west[1]) * inv_cos
        - north_wind * north_pair(north[1], south[1])
        + turning * north_wind
        - zonal_pair(east[0], west[0]) * inv_cos
    )
    rate_north = (
        -east_wind * zonal_pair(east[2], west[2]) * inv_cos
        - north_wind * north_pair(north[2], south[2])
        - turning * east_wind
        - north_pair(north[0], south[0])
    )
    return jnp.stack([rate_height, rate_east, rate_north], axis=0)


def second_step(state, halos, cos_two, sin_two, lon_step, lat_step, time_step):
    west_two, east_two, far_wide, near_row = halos
    _, rows, width = state.shape
    lat_index = lax.axis_index("lat")
    at_pole = lat_index == 0
    at_end = lat_index == lax.axis_size("lat") - 1
    flip = jnp.array([1.0, -1.0, -1.0], jnp.float32)[:, None]
    cos_all = cos_two[1:-1]
    sinlat = sin_two[2:-2][:, None]

    wide_rows = jnp.concatenate([west_two[:, :, 1:], state, east_two[:, :, :1]], axis=2)
    north_rows = lat_shift(wide_rows[:, rows - 2:, :], -1)
    south_rows = lat_shift(wide_rows[:, :2, :], 1)
    pole_rows = jnp.stack([far_wide[:, 1, :], far_wide[:, 0, :]], axis=1) * flip[:, :, None]
    north_rows = jnp.where(at_pole, pole_rows, north_rows)
    end_rows = jnp.concatenate([wide_rows[:, -1:, :], wide_rows[:, -1:, :]], axis=1)
    south_rows = jnp.where(at_end, end_rows, south_rows)

    rates_now = stencil(
        state, west_two[:, :, 1:], east_two[:, :, :1], north_rows[:, 1, 1:-1], south_rows[:, 0, 1:-1],
        cos_all, sinlat, lon_step, lat_step,
    )
    middle = state + 0.5 * time_step * rates_now

    def point(centre, east, west, north, south, cos_north, cos_south, coslat, sinlat):
        rate = point_rates(centre, east, west, north, south, cos_north, cos_south, coslat, sinlat, lon_step, lat_step)
        return centre + 0.5 * time_step * rate

    west_far, west_near = west_two[:, :, 0], west_two[:, :, 1]
    east_near, east_far = east_two[:, :, 0], east_two[:, :, 1]
    cos_rows, sin_rows = cos_two[2:-2], sin_two[2:-2]
    west_mid = point(
        west_near, state[:, :, 0], west_far,
        jnp.concatenate([north_rows[:, 1, 0:1], west_near[:, :-1]], axis=1),
        jnp.concatenate([west_near[:, 1:], south_rows[:, 0, 0:1]], axis=1),
        cos_two[1:-3], cos_two[3:-1], cos_rows, sin_rows,
    )[:, :, None]
    east_mid = point(
        east_near, east_far, state[:, :, width - 1],
        jnp.concatenate([north_rows[:, 1, width + 1:], east_near[:, :-1]], axis=1),
        jnp.concatenate([east_near[:, 1:], south_rows[:, 0, width + 1:]], axis=1),
        cos_two[1:-3], cos_two[3:-1], cos_rows, sin_rows,
    )[:, :, None]
    north_mid = point(
        north_rows[:, 1, 1:-1], north_rows[:, 1, 2:], north_rows[:, 1, :-2],
        north_rows[:, 0, 1:-1], state[:, 0, :],
        cos_two[0], cos_two[2], cos_two[1], sin_two[1],
    )
    south_mid = point(
        south_rows[:, 0, 1:-1], south_rows[:, 0, 2:], south_rows[:, 0, :-2],
        state[:, rows - 1, :], south_rows[:, 1, 1:-1],
        cos_two[rows + 1], cos_two[rows + 3], cos_two[rows + 2], sin_two[rows + 2],
    )
    far_mid = point(
        far_wide[:, 0, 1:-1], far_wide[:, 0, 2:], far_wide[:, 0, :-2],
        near_row[:, 1:-1] * flip, far_wide[:, 1, 1:-1],
        cos_two[1], cos_two[3], cos_two[2], sin_two[2],
    )
    north_mid = jnp.where(at_pole, far_mid * flip, north_mid)
    south_mid = jnp.where(at_end, middle[:, -1, :], south_mid)
    rates_now = stencil(
        middle, west_mid, east_mid, north_mid, south_mid, cos_all, sinlat, lon_step, lat_step
    )
    return state + time_step * rates_now


def shards(height, east_wind, north_wind, cutoffs):
    rows_here = height.shape[0]
    lat_index = lax.axis_index("lat")
    lat_step = math.pi / LAT_ROWS
    lon_step = 2.0 * math.pi / NLON
    time_step = COURANT * lat_step
    first_row = (lat_index * rows_here).astype(jnp.float32)
    index = first_row + jnp.arange(-2, rows_here + 2).astype(jnp.float32)
    cos_two = jnp.abs(jnp.sin((index + 0.5) * lat_step))
    sin_two = jnp.cos((index + 0.5) * lat_step)
    cos_all = cos_two[1:-1]
    sinlat = sin_two[2:-2][:, None]
    width = height.shape[1]
    table = local_table(0, width)
    wide_table = local_table(-2, width + 4)
    state = jnp.stack([height, east_wind, north_wind], axis=0)
    for step_index in range(STEPS):
        last = step_index == STEPS - 1
        if step_index == 0:
            rates_now = tendency(state, cos_all, sinlat, lon_step, lat_step)
            middle = state + 0.5 * time_step * rates_now
            rates_now = tendency(middle, cos_all, sinlat, lon_step, lat_step)
            advanced = state + time_step * rates_now
        else:
            advanced = second_step(state, halos, cos_two, sin_two, lon_step, lat_step, time_step)
        state, halos = filter_state(advanced, cutoffs, table, wide_table, not last)
    return (state[0], state[1], state[2])


def solution(mesh):
    placed = (P("lat", "lon"), P("lat", "lon"), P("lat", "lon"), P())
    return jax.shard_map(
        shards,
        mesh=mesh,
        in_specs=placed,
        out_specs=(P("lat", "lon"), P("lat", "lon"), P("lat", "lon")),
        check_vma=False,
    )
```

```python
import math

import jax
import jax.numpy as jnp
from jax import lax
from jax.sharding import PartitionSpec as P

NLON = 7200
LAT_ROWS = 3600
KMAX = 64
STEPS = 2


COURANT = 0.1
OMEGA_RATE = 1.5


def with_halo(value, sides, width, wrap):
    for axis, dim in sides:
        devices, length = (lax.axis_size(axis), value.shape[dim])
        up = [(i, (i + 1) % devices) for i in range(devices if wrap else devices - 1)]
        down = [(j, i) for i, j in up]
        last = lax.slice_in_dim(value, length - width, length, axis=dim)
        first = lax.slice_in_dim(value, 0, width, axis=dim)
        before = lax.ppermute(last, axis, up)
        after = lax.ppermute(first, axis, down)
        value = jnp.concatenate([before, value, after], axis=dim)
    return value


def from_behind(value, axis, by):
    devices = lax.axis_size(axis)
    return lax.ppermute(value, axis, [(i, (i + by) % devices) for i in range(devices)])


def lat_shift(value, by):
    devices = lax.axis_size("lat")
    pairs = [(i + by, i) for i in range(devices) if 0 <= i + by < devices]
    return lax.ppermute(value, "lat", pairs)


def local_table(first, width):
    waves = jnp.arange(KMAX + 1, dtype=jnp.int32)
    columns = (lax.axis_index("lon") * NLON // lax.axis_size("lon") + first) % NLON
    columns = (columns + jnp.arange(width, dtype=jnp.int32)) % NLON
    phase = waves[:, None] * columns[None, :] % NLON
    angle = phase.astype(jnp.float32) * (2.0 * math.pi / NLON)
    return jnp.concatenate([jnp.cos(angle), jnp.sin(angle)], axis=0)


def spectral_weights(cut_rows):
    waves = jnp.arange(KMAX + 1, dtype=jnp.int32)
    scale = jnp.where(waves == 0, 1.0 / NLON, 2.0 / NLON).astype(jnp.float32)
    keep = (waves[None, :] <= cut_rows[:, None]).astype(jnp.float32) * scale[None, :]
    return jnp.concatenate([keep, keep], axis=1)


def half_turn_signs():
    waves = jnp.arange(KMAX + 1, dtype=jnp.int32)
    signs = jnp.where(waves % 2 == 0, 1.0, -1.0).astype(jnp.float32)
    return jnp.concatenate([signs, signs], axis=0)


def project(fields, table):
    return jnp.einsum("fnw,kw->fnk", fields, table, precision=lax.Precision.HIGHEST)


def expand(coeffs, table):
    return jnp.einsum("fnk,kw->fnw", coeffs, table, precision=lax.Precision.HIGHEST)


def low_pass(fields, cut_rows, active, table, wide_table, with_halos):
    devices = lax.axis_size("lon")
    lon_index = lax.axis_index("lon")
    count, rows, width = fields.shape
    share = rows // devices
    partial = project(fields, table)
    modes = partial.shape[2]
    gathered = lax.all_to_all(partial, "lon", split_axis=1, concat_axis=0, tiled=True)
    reduced = gathered.reshape(devices, count, share, modes).sum(axis=0)
    payload = [jnp.broadcast_to(reduced.reshape(1, -1), (devices, count * share * modes))]
    if with_halos:
        targets = jnp.arange(devices, dtype=jnp.int32)[:, None]
        to_east = targets == (lon_index + 1) % devices
        edge = jnp.where(to_east, fields[:, :, -1].reshape(1, -1), fields[:, :, 0].reshape(1, -1))
        payload += [edge, jnp.broadcast_to(fields[:, 0, :].reshape(1, -1), (devices, count * width))]
    spread = lax.all_to_all(jnp.concatenate(payload, axis=1), "lon", split_axis=0, concat_axis=0, tiled=True)
    block = count * share * modes
    coeffs = spread[:, :block].reshape(devices, count, share, modes)
    coeffs = jnp.moveaxis(coeffs, 0, 1).reshape(count, rows, modes)
    weights = spectral_weights(cut_rows)
    scaled = coeffs * weights[None]
    if not with_halos:
        smooth = expand(scaled, table)
        return jnp.where(active[None, :, None], smooth, fields), None, None
    wide = expand(scaled, wide_table)
    smooth = wide[:, :, 1:-1]
    filtered = jnp.where(active[None, :, None], smooth, fields)
    edges = spread[:, block:block + count * rows].reshape(devices, count, rows)
    rows_far = spread[:, block + count * rows:].reshape(devices, count, width)
    west_raw = edges[(lon_index - 1) % devices]
    east_raw = edges[(lon_index + 1) % devices]
    far_raw = rows_far[(lon_index + devices // 2) % devices]
    west = jnp.where(active[None, :], wide[:, :, 0], west_raw)[:, :, None]
    east = jnp.where(active[None, :], wide[:, :, -1], east_raw)[:, :, None]
    far_wide = expand(scaled[:, :2, :] * half_turn_signs()[None, None, :], wide_table)
    far = jnp.where(active[0], far_wide[:, 0, 1:-1], far_raw)
    return filtered, (west, east, far), (far_wide, wide[:, 0, :])


def filter_state(state, cutoffs, table, wide_table, with_halos):
    rows_here = state.shape[1]
    lat_count = lax.axis_size("lat")
    lat_index = lax.axis_index("lat")
    filtered_rows = cutoffs.shape[0]
    cut_all = jnp.pad(cutoffs, (0, rows_here * lat_count - filtered_rows))
    global_rows = lat_index * rows_here + jnp.arange(rows_here, dtype=jnp.int32)
    cut_rows = lax.dynamic_slice_in_dim(cut_all, lat_index * rows_here, rows_here, 0)
    return low_pass(state, cut_rows, global_rows < filtered_rows, table, wide_table, with_halos)


def point_rates(centre, east, west, north, south, cos_north, cos_south, coslat, sinlat, lon_step, lat_step):
    def zonal_pair(east_value, west_value):
        return (east_value - west_value) * (0.5 / lon_step)

    def north_pair(north_value, south_value):
        return (north_value - south_value) * (0.5 / lat_step)

    height, east_wind, north_wind = (centre[0], centre[1], centre[2])
    inv_cos = 1.0 / coslat
    turning = 2.0 * OMEGA_RATE * sinlat + east_wind * sinlat * inv_cos
    flux_north = north[0] * north[2] * cos_north
    flux_south = south[0] * south[2] * cos_south
    rate_height = -(zonal_pair(east[0] * east[1], west[0] * west[1]) + north_pair(flux_north, flux_south)) * inv_cos
    rate_east = (
        -east_wind * zonal_pair(east[1], west[1]) * inv_cos
        - north_wind * north_pair(north[1], south[1])
        + turning * north_wind
        - zonal_pair(east[0], west[0]) * inv_cos
    )
    rate_north = (
        -east_wind * zonal_pair(east[2], west[2]) * inv_cos
        - north_wind * north_pair(north[2], south[2])
        - turning * east_wind
        - north_pair(north[0], south[0])
    )
    return jnp.stack([rate_height, rate_east, rate_north], axis=0)


def tendency(state, cos_all, sinlat, lon_step, lat_step, lon_halos=None, far=None):
    lat_index = lax.axis_index("lat")
    lat_count = lax.axis_size("lat")
    flips = jnp.array([1.0, -1.0, -1.0], jnp.float32)
    if lon_halos is None:
        edge_cols = jnp.concatenate([state[:, :, :1], state[:, :, -1:]], axis=2)
        got_cols = with_halo(edge_cols, (("lon", 2),), 1, True)
        west_col = got_cols[:, :, 0:1]
        east_col = got_cols[:, :, 3:4]
        if far is None:
            mirror = from_behind(state[:, 0, :], "lon", lax.axis_size("lon") // 2)
        else:
            mirror = far
    else:
        west_col, east_col, mirror = lon_halos
    mirror = mirror * flips[:, None]
    edge_rows = jnp.concatenate([state[:, :1, :], state[:, -1:, :]], axis=1)
    got_rows = with_halo(edge_rows, (("lat", 1),), 1, False)
    northmost = jnp.where(lat_index == 0, mirror, got_rows[:, 0, :])
    southmost = jnp.where(lat_index == lat_count - 1, state[:, -1, :], got_rows[:, 3, :])
    return stencil(state, west_col, east_col, northmost, southmost, cos_all, sinlat, lon_step, lat_step)


def stencil(state, west_col, east_col, northmost, southmost, cos_all, sinlat, lon_step, lat_step):
    corner = jnp.zeros((3, 1, 1), jnp.float32)
    top_line = jnp.concatenate([corner, northmost[:, None, :], corner], axis=2)
    bottom_line = jnp.concatenate([corner, southmost[:, None, :], corner], axis=2)
    middle_lines = jnp.concatenate([west_col, state, east_col], axis=2)
    extended = jnp.concatenate([top_line, middle_lines, bottom_line], axis=1)
    east_side = extended[:, 1:-1, 2:]
    west_side = extended[:, 1:-1, :-2]
    north_side = extended[:, :-2, 1:-1]
    south_side = extended[:, 2:, 1:-1]
    cos_north = cos_all[:-2][:, None]
    cos_south = cos_all[2:][:, None]
    coslat = cos_all[1:-1][:, None]

    def zonal_pair(east_value, west_value):
        return (east_value - west_value) * (0.5 / lon_step)

    def north_pair(north_value, south_value):
        return (north_value - south_value) * (0.5 / lat_step)

    height, east, north = (state[0], state[1], state[2])
    inv_cos = 1.0 / coslat
    turning = 2.0 * OMEGA_RATE * sinlat + east * sinlat * inv_cos
    flux_north = north_side[0] * north_side[2] * cos_north
    flux_south = south_side[0] * south_side[2] * cos_south
    rate_height = (
        -(
            zonal_pair(east_side[0] * east_side[1], west_side[0] * west_side[1])
            + north_pair(flux_north, flux_south)
        )
        * inv_cos
    )
    rate_east = (
        -east * zonal_pair(east_side[1], west_side[1]) * inv_cos
        - north * north_pair(north_side[1], south_side[1])
        + turning * north
        - zonal_pair(east_side[0], west_side[0]) * inv_cos
    )
    rate_north = (
        -east * zonal_pair(east_side[2], west_side[2]) * inv_cos
        - north * north_pair(north_side[2], south_side[2])
        - turning * east
        - north_pair(north_side[0], south_side[0])
    )
    return jnp.stack([rate_height, rate_east, rate_north], axis=0)


def second_step(state, lon_halos, pole, cos_two, sin_two, lon_step, lat_step, time_step):
    west_col, east_col, far_row = lon_halos
    far_wide, near_row = pole
    _, rows, width = state.shape
    lat_index = lax.axis_index("lat")
    at_pole = lat_index == 0
    at_end = lat_index == lax.axis_size("lat") - 1
    flip = jnp.array([1.0, -1.0, -1.0], jnp.float32)[:, None]
    cos_all = cos_two[1:-1]
    sinlat = sin_two[2:-2][:, None]

    wide_rows = jnp.concatenate([west_col, state, east_col], axis=2)
    north_rows = lat_shift(wide_rows[:, rows - 2:, :], -1)
    south_rows = lat_shift(wide_rows[:, :2, :], 1)
    pole_rows = jnp.stack([far_wide[:, 1, :], far_wide[:, 0, :]], axis=1) * flip[:, :, None]
    north_rows = jnp.where(at_pole, pole_rows, north_rows)
    end_rows = jnp.concatenate([wide_rows[:, -1:, :], wide_rows[:, -1:, :]], axis=1)
    south_rows = jnp.where(at_end, end_rows, south_rows)

    rates_now = stencil(
        state, west_col, east_col, north_rows[:, 1, 1:-1], south_rows[:, 0, 1:-1],
        cos_all, sinlat, lon_step, lat_step,
    )
    middle = state + 0.5 * time_step * rates_now

    def point(centre, east, west, north, south, cos_north, cos_south, coslat, sinlat):
        rate = point_rates(centre, east, west, north, south, cos_north, cos_south, coslat, sinlat, lon_step, lat_step)
        return centre + 0.5 * time_step * rate

    north_mid = point(
        north_rows[:, 1, 1:-1], north_rows[:, 1, 2:], north_rows[:, 1, :-2],
        north_rows[:, 0, 1:-1], state[:, 0, :],
        cos_two[0], cos_two[2], cos_two[1], sin_two[1],
    )
    south_mid = point(
        south_rows[:, 0, 1:-1], south_rows[:, 0, 2:], south_rows[:, 0, :-2],
        state[:, rows - 1, :], south_rows[:, 1, 1:-1],
        cos_two[rows + 1], cos_two[rows + 3], cos_two[rows + 2], sin_two[rows + 2],
    )
    far_mid = point(
        far_wide[:, 0, 1:-1], far_wide[:, 0, 2:], far_wide[:, 0, :-2],
        near_row[:, 1:-1] * flip, far_wide[:, 1, 1:-1],
        cos_two[1], cos_two[3], cos_two[2], sin_two[2],
    )
    north_mid = jnp.where(at_pole, far_mid * flip, north_mid)
    south_mid = jnp.where(at_end, middle[:, -1, :], south_mid)
    edge_cols = jnp.concatenate([middle[:, :, :1], middle[:, :, -1:]], axis=2)
    got_cols = with_halo(edge_cols, (("lon", 2),), 1, True)
    rates_now = stencil(
        middle, got_cols[:, :, 0:1], got_cols[:, :, 3:4], north_mid, south_mid,
        cos_all, sinlat, lon_step, lat_step,
    )
    return state + time_step * rates_now


def shards(height, east_wind, north_wind, cutoffs):
    rows_here = height.shape[0]
    lat_index = lax.axis_index("lat")
    lat_step = math.pi / LAT_ROWS
    lon_step = 2.0 * math.pi / NLON
    time_step = COURANT * lat_step
    first_row = (lat_index * rows_here).astype(jnp.float32)
    index = first_row + jnp.arange(-2, rows_here + 2).astype(jnp.float32)
    cos_two = jnp.abs(jnp.sin((index + 0.5) * lat_step))
    sin_two = jnp.cos((index + 0.5) * lat_step)
    cos_all = cos_two[1:-1]
    sinlat = sin_two[2:-2][:, None]
    width = height.shape[1]
    table = local_table(0, width)
    wide_table = local_table(-1, width + 2)
    state = jnp.stack([height, east_wind, north_wind], axis=0)
    for step_index in range(STEPS):
        last = step_index == STEPS - 1
        if step_index == 0:
            rates_now = tendency(state, cos_all, sinlat, lon_step, lat_step)
            middle = state + 0.5 * time_step * rates_now
            rates_now = tendency(middle, cos_all, sinlat, lon_step, lat_step)
            advanced = state + time_step * rates_now
        else:
            advanced = second_step(state, lon_halos, pole, cos_two, sin_two, lon_step, lat_step, time_step)
        state, lon_halos, pole = filter_state(advanced, cutoffs, table, wide_table, not last)
    return (state[0], state[1], state[2])


def solution(mesh):
    placed = (P("lat", "lon"), P("lat", "lon"), P("lat", "lon"), P())
    return jax.shard_map(
        shards,
        mesh=mesh,
        in_specs=placed,
        out_specs=(P("lat", "lon"), P("lat", "lon"), P("lat", "lon")),
        check_vma=False,
    )
```

```python
import math

import jax
import jax.numpy as jnp
from jax import lax
from jax.sharding import PartitionSpec as P

NLON = 7200
LAT_ROWS = 3600
KMAX = 64
STEPS = 2


COURANT = 0.1
OMEGA_RATE = 1.5


def with_halo(value, sides, width, wrap):
    for axis, dim in sides:
        devices, length = (lax.axis_size(axis), value.shape[dim])
        up = [(i, (i + 1) % devices) for i in range(devices if wrap else devices - 1)]
        down = [(j, i) for i, j in up]
        last = lax.slice_in_dim(value, length - width, length, axis=dim)
        first = lax.slice_in_dim(value, 0, width, axis=dim)
        before = lax.ppermute(last, axis, up)
        after = lax.ppermute(first, axis, down)
        value = jnp.concatenate([before, value, after], axis=dim)
    return value


def from_behind(value, axis, by):
    devices = lax.axis_size(axis)
    return lax.ppermute(value, axis, [(i, (i + by) % devices) for i in range(devices)])


def local_table(first, width):
    waves = jnp.arange(KMAX + 1, dtype=jnp.int32)
    columns = (lax.axis_index("lon") * NLON // lax.axis_size("lon") + first) % NLON
    columns = (columns + jnp.arange(width, dtype=jnp.int32)) % NLON
    phase = waves[:, None] * columns[None, :] % NLON
    angle = phase.astype(jnp.float32) * (2.0 * math.pi / NLON)
    return jnp.concatenate([jnp.cos(angle), jnp.sin(angle)], axis=0)


def spectral_weights(cut_rows):
    waves = jnp.arange(KMAX + 1, dtype=jnp.int32)
    scale = jnp.where(waves == 0, 1.0 / NLON, 2.0 / NLON).astype(jnp.float32)
    keep = (waves[None, :] <= cut_rows[:, None]).astype(jnp.float32) * scale[None, :]
    return jnp.concatenate([keep, keep], axis=1)


def half_turn_signs():
    waves = jnp.arange(KMAX + 1, dtype=jnp.int32)
    signs = jnp.where(waves % 2 == 0, 1.0, -1.0).astype(jnp.float32)
    return jnp.concatenate([signs, signs], axis=0)


def project(fields, table):
    return jnp.einsum("fnw,kw->fnk", fields, table, precision=lax.Precision.HIGHEST)


def expand(coeffs, table):
    return jnp.einsum("fnk,kw->fnw", coeffs, table, precision=lax.Precision.HIGHEST)


def low_pass(fields, cut_rows, active, table, wide_table, with_halos):
    devices = lax.axis_size("lon")
    lon_index = lax.axis_index("lon")
    count, rows, width = fields.shape
    share = rows // devices
    partial = project(fields, table)
    modes = partial.shape[2]
    gathered = lax.all_to_all(partial, "lon", split_axis=1, concat_axis=0, tiled=True)
    reduced = gathered.reshape(devices, count, share, modes).sum(axis=0)
    payload = [jnp.broadcast_to(reduced.reshape(1, -1), (devices, count * share * modes))]
    if with_halos:
        targets = jnp.arange(devices, dtype=jnp.int32)[:, None]
        to_east = targets == (lon_index + 1) % devices
        edge = jnp.where(to_east, fields[:, :, -1].reshape(1, -1), fields[:, :, 0].reshape(1, -1))
        payload += [edge]
    spread = lax.all_to_all(jnp.concatenate(payload, axis=1), "lon", split_axis=0, concat_axis=0, tiled=True)
    block = count * share * modes
    coeffs = spread[:, :block].reshape(devices, count, share, modes)
    coeffs = jnp.moveaxis(coeffs, 0, 1).reshape(count, rows, modes)
    weights = spectral_weights(cut_rows)
    scaled = coeffs * weights[None]
    if not with_halos:
        smooth = expand(scaled, table)
        return jnp.where(active[None, :, None], smooth, fields), None, None
    wide = expand(scaled, wide_table)
    smooth = wide[:, :, 1:-1]
    filtered = jnp.where(active[None, :, None], smooth, fields)
    edges = spread[:, block:].reshape(devices, count, rows)
    west_raw = edges[(lon_index - 1) % devices]
    east_raw = edges[(lon_index + 1) % devices]
    west = jnp.where(active[None, :], wide[:, :, 0], west_raw)[:, :, None]
    east = jnp.where(active[None, :], wide[:, :, -1], east_raw)[:, :, None]
    far_wide = expand(scaled[:, :2, :] * half_turn_signs()[None, None, :], wide_table)
    far = far_wide[:, 0, 1:-1]
    return filtered, (west, east, far), (far_wide, wide[:, 0, :])


def filter_state(state, cutoffs, table, wide_table, with_halos):
    rows_here = state.shape[1]
    lat_count = lax.axis_size("lat")
    lat_index = lax.axis_index("lat")
    filtered_rows = cutoffs.shape[0]
    cut_all = jnp.pad(cutoffs, (0, rows_here * lat_count - filtered_rows))
    global_rows = lat_index * rows_here + jnp.arange(rows_here, dtype=jnp.int32)
    cut_rows = lax.dynamic_slice_in_dim(cut_all, lat_index * rows_here, rows_here, 0)
    return low_pass(state, cut_rows, global_rows < filtered_rows, table, wide_table, with_halos)


def rates(ext, cos_all, sinlat, lon_step, lat_step):
    east_side = ext[:, 1:-1, 2:]
    west_side = ext[:, 1:-1, :-2]
    north_side = ext[:, :-2, 1:-1]
    south_side = ext[:, 2:, 1:-1]
    cos_north = cos_all[:-2][:, None]
    cos_south = cos_all[2:][:, None]
    coslat = cos_all[1:-1][:, None]
    sinlat = sinlat[:, None]

    def zonal_pair(east_value, west_value):
        return (east_value - west_value) * (0.5 / lon_step)

    def north_pair(north_value, south_value):
        return (north_value - south_value) * (0.5 / lat_step)

    centre = ext[:, 1:-1, 1:-1]
    height, east, north = (centre[0], centre[1], centre[2])
    inv_cos = 1.0 / coslat
    turning = 2.0 * OMEGA_RATE * sinlat + east * sinlat * inv_cos
    flux_north = north_side[0] * north_side[2] * cos_north
    flux_south = south_side[0] * south_side[2] * cos_south
    rate_height = (
        -(
            zonal_pair(east_side[0] * east_side[1], west_side[0] * west_side[1])
            + north_pair(flux_north, flux_south)
        )
        * inv_cos
    )
    rate_east = (
        -east * zonal_pair(east_side[1], west_side[1]) * inv_cos
        - north * north_pair(north_side[1], south_side[1])
        + turning * north
        - zonal_pair(east_side[0], west_side[0]) * inv_cos
    )
    rate_north = (
        -east * zonal_pair(east_side[2], west_side[2]) * inv_cos
        - north * north_pair(north_side[2], south_side[2])
        - turning * east
        - north_pair(north_side[0], south_side[0])
    )
    return jnp.stack([rate_height, rate_east, rate_north], axis=0)


def tendency(state, cos_all, sinlat, lon_step, lat_step, lon_halos=None, far=None):
    lat_index = lax.axis_index("lat")
    lat_count = lax.axis_size("lat")
    flips = jnp.array([1.0, -1.0, -1.0], jnp.float32)
    if lon_halos is None:
        edge_cols = jnp.concatenate([state[:, :, :1], state[:, :, -1:]], axis=2)
        got_cols = with_halo(edge_cols, (("lon", 2),), 1, True)
        west_col = got_cols[:, :, 0:1]
        east_col = got_cols[:, :, 3:4]
        if far is None:
            mirror = from_behind(state[:, 0, :], "lon", lax.axis_size("lon") // 2)
        else:
            mirror = far
    else:
        west_col, east_col, mirror = lon_halos
    mirror = mirror * flips[:, None]
    edge_rows = jnp.concatenate([state[:, :1, :], state[:, -1:, :]], axis=1)
    got_rows = with_halo(edge_rows, (("lat", 1),), 1, False)
    northmost = jnp.where(lat_index == 0, mirror, got_rows[:, 0, :])
    southmost = jnp.where(lat_index == lat_count - 1, state[:, -1, :], got_rows[:, 3, :])
    corner = jnp.zeros((3, 1, 1), jnp.float32)
    top_line = jnp.concatenate([corner, northmost[:, None, :], corner], axis=2)
    bottom_line = jnp.concatenate([corner, southmost[:, None, :], corner], axis=2)
    middle_lines = jnp.concatenate([west_col, state, east_col], axis=2)
    extended = jnp.concatenate([top_line, middle_lines, bottom_line], axis=1)
    east_side = extended[:, 1:-1, 2:]
    west_side = extended[:, 1:-1, :-2]
    north_side = extended[:, :-2, 1:-1]
    south_side = extended[:, 2:, 1:-1]
    cos_north = cos_all[:-2][:, None]
    cos_south = cos_all[2:][:, None]
    coslat = cos_all[1:-1][:, None]

    def zonal_pair(east_value, west_value):
        return (east_value - west_value) * (0.5 / lon_step)

    def north_pair(north_value, south_value):
        return (north_value - south_value) * (0.5 / lat_step)

    height, east, north = (state[0], state[1], state[2])
    inv_cos = 1.0 / coslat
    turning = 2.0 * OMEGA_RATE * sinlat + east * sinlat * inv_cos
    flux_north = north_side[0] * north_side[2] * cos_north
    flux_south = south_side[0] * south_side[2] * cos_south
    rate_height = (
        -(
            zonal_pair(east_side[0] * east_side[1], west_side[0] * west_side[1])
            + north_pair(flux_north, flux_south)
        )
        * inv_cos
    )
    rate_east = (
        -east * zonal_pair(east_side[1], west_side[1]) * inv_cos
        - north * north_pair(north_side[1], south_side[1])
        + turning * north
        - zonal_pair(east_side[0], west_side[0]) * inv_cos
    )
    rate_north = (
        -east * zonal_pair(east_side[2], west_side[2]) * inv_cos
        - north * north_pair(north_side[2], south_side[2])
        - turning * east
        - north_pair(north_side[0], south_side[0])
    )
    return jnp.stack([rate_height, rate_east, rate_north], axis=0)


def shards(height, east_wind, north_wind, cutoffs):
    rows_here = height.shape[0]
    lat_index = lax.axis_index("lat")
    lat_step = math.pi / LAT_ROWS
    lon_step = 2.0 * math.pi / NLON
    time_step = COURANT * lat_step
    first_row = (lat_index * rows_here).astype(jnp.float32)
    index = first_row + jnp.arange(-1, rows_here + 1).astype(jnp.float32)
    cos_all = jnp.abs(jnp.sin((index + 0.5) * lat_step))
    sin_all = jnp.cos((index + 0.5) * lat_step)
    sinlat = sin_all[1:-1][:, None]
    width = height.shape[1]
    table = local_table(0, width)
    wide_table = local_table(-1, width + 2)
    state = jnp.stack([height, east_wind, north_wind], axis=0)
    lon_halos = None
    pole = None
    flips = jnp.array([1.0, -1.0, -1.0], jnp.float32)[:, None]
    for step_index in range(STEPS):
        rates_now = tendency(state, cos_all, sinlat, lon_step, lat_step, lon_halos)
        middle = state + 0.5 * time_step * rates_now
        far = None
        if pole is not None:
            far_wide, near_row = pole
            far_box = jnp.stack([near_row * flips, far_wide[:, 0, :], far_wide[:, 1, :]], axis=1)
            far_rate = rates(far_box, cos_all[0:3], sin_all[1:2], lon_step, lat_step)[:, 0, :]
            far = far_wide[:, 0, 1:-1] + 0.5 * time_step * far_rate
        rates_now = tendency(middle, cos_all, sinlat, lon_step, lat_step, None, far)
        advanced = state + time_step * rates_now
        last = step_index == STEPS - 1
        state, lon_halos, pole = filter_state(advanced, cutoffs, table, wide_table, not last)
    return (state[0], state[1], state[2])


def solution(mesh):
    placed = (P("lat", "lon"), P("lat", "lon"), P("lat", "lon"), P())
    return jax.shard_map(
        shards,
        mesh=mesh,
        in_specs=placed,
        out_specs=(P("lat", "lon"), P("lat", "lon"), P("lat", "lon")),
        check_vma=False,
    )
```

```python
import math

import jax
import jax.numpy as jnp
from jax import lax
from jax.sharding import PartitionSpec as P

NLON = 7200
LAT_ROWS = 3600
KMAX = 64
STEPS = 2


COURANT = 0.1
OMEGA_RATE = 1.5


def with_halo(value, sides, width, wrap):
    for axis, dim in sides:
        devices, length = (lax.axis_size(axis), value.shape[dim])
        up = [(i, (i + 1) % devices) for i in range(devices if wrap else devices - 1)]
        down = [(j, i) for i, j in up]
        last = lax.slice_in_dim(value, length - width, length, axis=dim)
        first = lax.slice_in_dim(value, 0, width, axis=dim)
        before = lax.ppermute(last, axis, up)
        after = lax.ppermute(first, axis, down)
        value = jnp.concatenate([before, value, after], axis=dim)
    return value


def from_behind(value, axis, by):
    devices = lax.axis_size(axis)
    return lax.ppermute(value, axis, [(i, (i + by) % devices) for i in range(devices)])


def local_table(first, width):
    waves = jnp.arange(KMAX + 1, dtype=jnp.int32)
    columns = (lax.axis_index("lon") * NLON // lax.axis_size("lon") + first) % NLON
    columns = (columns + jnp.arange(width, dtype=jnp.int32)) % NLON
    phase = waves[:, None] * columns[None, :] % NLON
    angle = phase.astype(jnp.float32) * (2.0 * math.pi / NLON)
    return jnp.concatenate([jnp.cos(angle), jnp.sin(angle)], axis=0)


def spectral_weights(cut_rows):
    waves = jnp.arange(KMAX + 1, dtype=jnp.int32)
    scale = jnp.where(waves == 0, 1.0 / NLON, 2.0 / NLON).astype(jnp.float32)
    keep = (waves[None, :] <= cut_rows[:, None]).astype(jnp.float32) * scale[None, :]
    return jnp.concatenate([keep, keep], axis=1)


def half_turn_signs():
    waves = jnp.arange(KMAX + 1, dtype=jnp.int32)
    signs = jnp.where(waves % 2 == 0, 1.0, -1.0).astype(jnp.float32)
    return jnp.concatenate([signs, signs], axis=0)


def project(fields, table):
    return jnp.einsum("fnw,kw->fnk", fields, table, precision=lax.Precision.HIGH)


def expand(coeffs, table):
    return jnp.einsum("fnk,kw->fnw", coeffs, table, precision=lax.Precision.HIGH)


def low_pass(fields, cut_rows, active, table, wide_table, with_halos):
    devices = lax.axis_size("lon")
    lon_index = lax.axis_index("lon")
    count, rows, width = fields.shape
    share = rows // devices
    partial = project(fields, table)
    modes = partial.shape[2]
    gathered = lax.all_to_all(partial, "lon", split_axis=1, concat_axis=0, tiled=True)
    reduced = gathered.reshape(devices, count, share, modes).sum(axis=0)
    payload = [jnp.broadcast_to(reduced.reshape(1, -1), (devices, count * share * modes))]
    if with_halos:
        targets = jnp.arange(devices, dtype=jnp.int32)[:, None]
        to_east = targets == (lon_index + 1) % devices
        edge = jnp.where(to_east, fields[:, :, -1].reshape(1, -1), fields[:, :, 0].reshape(1, -1))
        payload += [edge, jnp.broadcast_to(fields[:, 0, :].reshape(1, -1), (devices, count * width))]
    spread = lax.all_to_all(jnp.concatenate(payload, axis=1), "lon", split_axis=0, concat_axis=0, tiled=True)
    block = count * share * modes
    coeffs = spread[:, :block].reshape(devices, count, share, modes)
    coeffs = jnp.moveaxis(coeffs, 0, 1).reshape(count, rows, modes)
    weights = spectral_weights(cut_rows)
    scaled = coeffs * weights[None]
    if not with_halos:
        smooth = expand(scaled, table)
        return jnp.where(active[None, :, None], smooth, fields), None, None
    wide = expand(scaled, wide_table)
    smooth = wide[:, :, 1:-1]
    filtered = jnp.where(active[None, :, None], smooth, fields)
    edges = spread[:, block:block + count * rows].reshape(devices, count, rows)
    rows_far = spread[:, block + count * rows:].reshape(devices, count, width)
    west_raw = edges[(lon_index - 1) % devices]
    east_raw = edges[(lon_index + 1) % devices]
    far_raw = rows_far[(lon_index + devices // 2) % devices]
    west = jnp.where(active[None, :], wide[:, :, 0], west_raw)[:, :, None]
    east = jnp.where(active[None, :], wide[:, :, -1], east_raw)[:, :, None]
    far_wide = expand(scaled[:, :2, :] * half_turn_signs()[None, None, :], wide_table)
    far = jnp.where(active[0], far_wide[:, 0, 1:-1], far_raw)
    return filtered, (west, east, far), (far_wide, wide[:, 0, :])


def filter_state(state, cutoffs, table, wide_table, with_halos):
    rows_here = state.shape[1]
    lat_count = lax.axis_size("lat")
    lat_index = lax.axis_index("lat")
    filtered_rows = cutoffs.shape[0]
    cut_all = jnp.pad(cutoffs, (0, rows_here * lat_count - filtered_rows))
    global_rows = lat_index * rows_here + jnp.arange(rows_here, dtype=jnp.int32)
    cut_rows = lax.dynamic_slice_in_dim(cut_all, lat_index * rows_here, rows_here, 0)
    return low_pass(state, cut_rows, global_rows < filtered_rows, table, wide_table, with_halos)


def rates(ext, cos_all, sinlat, lon_step, lat_step):
    east_side = ext[:, 1:-1, 2:]
    west_side = ext[:, 1:-1, :-2]
    north_side = ext[:, :-2, 1:-1]
    south_side = ext[:, 2:, 1:-1]
    cos_north = cos_all[:-2][:, None]
    cos_south = cos_all[2:][:, None]
    coslat = cos_all[1:-1][:, None]
    sinlat = sinlat[:, None]

    def zonal_pair(east_value, west_value):
        return (east_value - west_value) * (0.5 / lon_step)

    def north_pair(north_value, south_value):
        return (north_value - south_value) * (0.5 / lat_step)

    centre = ext[:, 1:-1, 1:-1]
    height, east, north = (centre[0], centre[1], centre[2])
    inv_cos = 1.0 / coslat
    turning = 2.0 * OMEGA_RATE * sinlat + east * sinlat * inv_cos
    flux_north = north_side[0] * north_side[2] * cos_north
    flux_south = south_side[0] * south_side[2] * cos_south
    rate_height = (
        -(
            zonal_pair(east_side[0] * east_side[1], west_side[0] * west_side[1])
            + north_pair(flux_north, flux_south)
        )
        * inv_cos
    )
    rate_east = (
        -east * zonal_pair(east_side[1], west_side[1]) * inv_cos
        - north * north_pair(north_side[1], south_side[1])
        + turning * north
        - zonal_pair(east_side[0], west_side[0]) * inv_cos
    )
    rate_north = (
        -east * zonal_pair(east_side[2], west_side[2]) * inv_cos
        - north * north_pair(north_side[2], south_side[2])
        - turning * east
        - north_pair(north_side[0], south_side[0])
    )
    return jnp.stack([rate_height, rate_east, rate_north], axis=0)


def tendency(state, cos_all, sinlat, lon_step, lat_step, lon_halos=None, far=None):
    lat_index = lax.axis_index("lat")
    lat_count = lax.axis_size("lat")
    flips = jnp.array([1.0, -1.0, -1.0], jnp.float32)
    if lon_halos is None:
        edge_cols = jnp.concatenate([state[:, :, :1], state[:, :, -1:]], axis=2)
        got_cols = with_halo(edge_cols, (("lon", 2),), 1, True)
        west_col = got_cols[:, :, 0:1]
        east_col = got_cols[:, :, 3:4]
        if far is None:
            mirror = from_behind(state[:, 0, :], "lon", lax.axis_size("lon") // 2)
        else:
            mirror = far
    else:
        west_col, east_col, mirror = lon_halos
    mirror = mirror * flips[:, None]
    edge_rows = jnp.concatenate([state[:, :1, :], state[:, -1:, :]], axis=1)
    got_rows = with_halo(edge_rows, (("lat", 1),), 1, False)
    northmost = jnp.where(lat_index == 0, mirror, got_rows[:, 0, :])
    southmost = jnp.where(lat_index == lat_count - 1, state[:, -1, :], got_rows[:, 3, :])
    corner = jnp.zeros((3, 1, 1), jnp.float32)
    top_line = jnp.concatenate([corner, northmost[:, None, :], corner], axis=2)
    bottom_line = jnp.concatenate([corner, southmost[:, None, :], corner], axis=2)
    middle_lines = jnp.concatenate([west_col, state, east_col], axis=2)
    extended = jnp.concatenate([top_line, middle_lines, bottom_line], axis=1)
    east_side = extended[:, 1:-1, 2:]
    west_side = extended[:, 1:-1, :-2]
    north_side = extended[:, :-2, 1:-1]
    south_side = extended[:, 2:, 1:-1]
    cos_north = cos_all[:-2][:, None]
    cos_south = cos_all[2:][:, None]
    coslat = cos_all[1:-1][:, None]

    def zonal_pair(east_value, west_value):
        return (east_value - west_value) * (0.5 / lon_step)

    def north_pair(north_value, south_value):
        return (north_value - south_value) * (0.5 / lat_step)

    height, east, north = (state[0], state[1], state[2])
    inv_cos = 1.0 / coslat
    turning = 2.0 * OMEGA_RATE * sinlat + east * sinlat * inv_cos
    flux_north = north_side[0] * north_side[2] * cos_north
    flux_south = south_side[0] * south_side[2] * cos_south
    rate_height = (
        -(
            zonal_pair(east_side[0] * east_side[1], west_side[0] * west_side[1])
            + north_pair(flux_north, flux_south)
        )
        * inv_cos
    )
    rate_east = (
        -east * zonal_pair(east_side[1], west_side[1]) * inv_cos
        - north * north_pair(north_side[1], south_side[1])
        + turning * north
        - zonal_pair(east_side[0], west_side[0]) * inv_cos
    )
    rate_north = (
        -east * zonal_pair(east_side[2], west_side[2]) * inv_cos
        - north * north_pair(north_side[2], south_side[2])
        - turning * east
        - north_pair(north_side[0], south_side[0])
    )
    return jnp.stack([rate_height, rate_east, rate_north], axis=0)


def shards(height, east_wind, north_wind, cutoffs):
    rows_here = height.shape[0]
    lat_index = lax.axis_index("lat")
    lat_step = math.pi / LAT_ROWS
    lon_step = 2.0 * math.pi / NLON
    time_step = COURANT * lat_step
    first_row = (lat_index * rows_here).astype(jnp.float32)
    index = first_row + jnp.arange(-1, rows_here + 1).astype(jnp.float32)
    cos_all = jnp.abs(jnp.sin((index + 0.5) * lat_step))
    sin_all = jnp.cos((index + 0.5) * lat_step)
    sinlat = sin_all[1:-1][:, None]
    width = height.shape[1]
    table = local_table(0, width)
    wide_table = local_table(-1, width + 2)
    state = jnp.stack([height, east_wind, north_wind], axis=0)
    lon_halos = None
    pole = None
    flips = jnp.array([1.0, -1.0, -1.0], jnp.float32)[:, None]
    for step_index in range(STEPS):
        rates_now = tendency(state, cos_all, sinlat, lon_step, lat_step, lon_halos)
        middle = state + 0.5 * time_step * rates_now
        far = None
        if pole is not None:
            far_wide, near_row = pole
            far_box = jnp.stack([near_row * flips, far_wide[:, 0, :], far_wide[:, 1, :]], axis=1)
            far_rate = rates(far_box, cos_all[0:3], sin_all[1:2], lon_step, lat_step)[:, 0, :]
            far = far_wide[:, 0, 1:-1] + 0.5 * time_step * far_rate
        rates_now = tendency(middle, cos_all, sinlat, lon_step, lat_step, None, far)
        advanced = state + time_step * rates_now
        last = step_index == STEPS - 1
        state, lon_halos, pole = filter_state(advanced, cutoffs, table, wide_table, not last)
    return (state[0], state[1], state[2])


def solution(mesh):
    placed = (P("lat", "lon"), P("lat", "lon"), P("lat", "lon"), P())
    return jax.shard_map(
        shards,
        mesh=mesh,
        in_specs=placed,
        out_specs=(P("lat", "lon"), P("lat", "lon"), P("lat", "lon")),
        check_vma=False,
    )
```

```python
import math

import jax
import jax.numpy as jnp
from jax import lax
from jax.sharding import PartitionSpec as P

NLON = 7200
LAT_ROWS = 3600
KMAX = 64
STEPS = 2


COURANT = 0.1
OMEGA_RATE = 1.5


def with_halo(value, sides, width, wrap):
    for axis, dim in sides:
        devices, length = (lax.axis_size(axis), value.shape[dim])
        up = [(i, (i + 1) % devices) for i in range(devices if wrap else devices - 1)]
        down = [(j, i) for i, j in up]
        last = lax.slice_in_dim(value, length - width, length, axis=dim)
        first = lax.slice_in_dim(value, 0, width, axis=dim)
        before = lax.ppermute(last, axis, up)
        after = lax.ppermute(first, axis, down)
        value = jnp.concatenate([before, value, after], axis=dim)
    return value


def from_behind(value, axis, by):
    devices = lax.axis_size(axis)
    return lax.ppermute(value, axis, [(i, (i + by) % devices) for i in range(devices)])


def local_table(first, width):
    waves = jnp.arange(KMAX + 1, dtype=jnp.int32)
    columns = (lax.axis_index("lon") * NLON // lax.axis_size("lon") + first) % NLON
    columns = (columns + jnp.arange(width, dtype=jnp.int32)) % NLON
    phase = waves[:, None] * columns[None, :] % NLON
    angle = phase.astype(jnp.float32) * (2.0 * math.pi / NLON)
    return jnp.concatenate([jnp.cos(angle), jnp.sin(angle)], axis=0)


def spectral_weights(cut_rows):
    waves = jnp.arange(KMAX + 1, dtype=jnp.int32)
    scale = jnp.where(waves == 0, 1.0 / NLON, 2.0 / NLON).astype(jnp.float32)
    keep = (waves[None, :] <= cut_rows[:, None]).astype(jnp.float32) * scale[None, :]
    return jnp.concatenate([keep, keep], axis=1)


def half_turn_signs():
    waves = jnp.arange(KMAX + 1, dtype=jnp.int32)
    signs = jnp.where(waves % 2 == 0, 1.0, -1.0).astype(jnp.float32)
    return jnp.concatenate([signs, signs], axis=0)


def project(fields, table):
    return jnp.einsum("fnw,kw->fnk", fields, table, precision=lax.Precision.HIGH)


def expand(coeffs, table):
    return jnp.einsum("fnk,kw->fnw", coeffs, table, precision=lax.Precision.HIGH)


def low_pass(fields, cut_rows, active, table, wide_table, with_halos):
    devices = lax.axis_size("lon")
    lon_index = lax.axis_index("lon")
    count, rows, width = fields.shape
    share = rows // devices
    partial = project(fields, table)
    modes = partial.shape[2]
    gathered = lax.all_to_all(partial, "lon", split_axis=1, concat_axis=0, tiled=True)
    reduced = gathered.reshape(devices, count, share, modes).sum(axis=0)
    payload = [jnp.broadcast_to(reduced.reshape(1, -1), (devices, count * share * modes))]
    if with_halos:
        targets = jnp.arange(devices, dtype=jnp.int32)[:, None]
        to_east = targets == (lon_index + 1) % devices
        edge = jnp.where(to_east, fields[:, :, -1].reshape(1, -1), fields[:, :, 0].reshape(1, -1))
        payload += [edge, jnp.broadcast_to(fields[:, 0, :].reshape(1, -1), (devices, count * width))]
    spread = lax.all_to_all(jnp.concatenate(payload, axis=1), "lon", split_axis=0, concat_axis=0, tiled=True)
    block = count * share * modes
    coeffs = spread[:, :block].reshape(devices, count, share, modes)
    coeffs = jnp.moveaxis(coeffs, 0, 1).reshape(count, rows, modes)
    weights = spectral_weights(cut_rows)
    scaled = coeffs * weights[None]
    if not with_halos:
        smooth = expand(scaled, table)
        return jnp.where(active[None, :, None], smooth, fields), None, None
    wide = expand(scaled, wide_table)
    smooth = wide[:, :, 1:-1]
    filtered = jnp.where(active[None, :, None], smooth, fields)
    edges = spread[:, block:block + count * rows].reshape(devices, count, rows)
    rows_far = spread[:, block + count * rows:].reshape(devices, count, width)
    west_raw = edges[(lon_index - 1) % devices]
    east_raw = edges[(lon_index + 1) % devices]
    far_raw = rows_far[(lon_index + devices // 2) % devices]
    west = jnp.where(active[None, :], wide[:, :, 0], west_raw)[:, :, None]
    east = jnp.where(active[None, :], wide[:, :, -1], east_raw)[:, :, None]
    far_wide = expand(scaled[:, :2, :] * half_turn_signs()[None, None, :], wide_table)
    far = jnp.where(active[0], far_wide[:, 0, 1:-1], far_raw)
    return filtered, (west, east, far), (far_wide, wide[:, 0, :])


def filter_state(state, cutoffs, table, wide_table, with_halos):
    rows_here = state.shape[1]
    lat_count = lax.axis_size("lat")
    lat_index = lax.axis_index("lat")
    filtered_rows = cutoffs.shape[0]
    cut_all = jnp.pad(cutoffs, (0, rows_here * lat_count - filtered_rows))
    global_rows = lat_index * rows_here + jnp.arange(rows_here, dtype=jnp.int32)
    cut_rows = lax.dynamic_slice_in_dim(cut_all, lat_index * rows_here, rows_here, 0)
    return low_pass(state, cut_rows, global_rows < filtered_rows, table, wide_table, with_halos)


def rates(ext, cos_all, sinlat, lon_step, lat_step):
    east_side = ext[:, 1:-1, 2:]
    west_side = ext[:, 1:-1, :-2]
    north_side = ext[:, :-2, 1:-1]
    south_side = ext[:, 2:, 1:-1]
    cos_north = cos_all[:-2][:, None]
    cos_south = cos_all[2:][:, None]
    coslat = cos_all[1:-1][:, None]
    sinlat = sinlat[:, None]

    def zonal_pair(east_value, west_value):
        return (east_value - west_value) * (0.5 / lon_step)

    def north_pair(north_value, south_value):
        return (north_value - south_value) * (0.5 / lat_step)

    centre = ext[:, 1:-1, 1:-1]
    height, east, north = (centre[0], centre[1], centre[2])
    inv_cos = 1.0 / coslat
    turning = 2.0 * OMEGA_RATE * sinlat + east * sinlat * inv_cos
    flux_north = north_side[0] * north_side[2] * cos_north
    flux_south = south_side[0] * south_side[2] * cos_south
    rate_height = (
        -(
            zonal_pair(east_side[0] * east_side[1], west_side[0] * west_side[1])
            + north_pair(flux_north, flux_south)
        )
        * inv_cos
    )
    rate_east = (
        -east * zonal_pair(east_side[1], west_side[1]) * inv_cos
        - north * north_pair(north_side[1], south_side[1])
        + turning * north
        - zonal_pair(east_side[0], west_side[0]) * inv_cos
    )
    rate_north = (
        -east * zonal_pair(east_side[2], west_side[2]) * inv_cos
        - north * north_pair(north_side[2], south_side[2])
        - turning * east
        - north_pair(north_side[0], south_side[0])
    )
    return jnp.stack([rate_height, rate_east, rate_north], axis=0)


def tendency(state, cos_all, sinlat, lon_step, lat_step, lon_halos=None, far=None):
    lat_index = lax.axis_index("lat")
    lat_count = lax.axis_size("lat")
    flips = jnp.array([1.0, -1.0, -1.0], jnp.float32)
    if lon_halos is None:
        edge_cols = jnp.concatenate([state[:, :, :1], state[:, :, -1:]], axis=2)
        got_cols = with_halo(edge_cols, (("lon", 2),), 1, True)
        west_col = got_cols[:, :, 0:1]
        east_col = got_cols[:, :, 3:4]
        if far is None:
            mirror = from_behind(state[:, 0, :], "lon", lax.axis_size("lon") // 2)
        else:
            mirror = far
    else:
        west_col, east_col, mirror = lon_halos
    mirror = mirror * flips[:, None]
    edge_rows = jnp.concatenate([state[:, :1, :], state[:, -1:, :]], axis=1)
    got_rows = with_halo(edge_rows, (("lat", 1),), 1, False)
    northmost = jnp.where(lat_index == 0, mirror, got_rows[:, 0, :])
    southmost = jnp.where(lat_index == lat_count - 1, state[:, -1, :], got_rows[:, 3, :])
    corner = jnp.zeros((3, 1, 1), jnp.float32)
    top_line = jnp.concatenate([corner, northmost[:, None, :], corner], axis=2)
    bottom_line = jnp.concatenate([corner, southmost[:, None, :], corner], axis=2)
    middle_lines = jnp.concatenate([west_col, state, east_col], axis=2)
    extended = jnp.concatenate([top_line, middle_lines, bottom_line], axis=1)
    east_side = extended[:, 1:-1, 2:]
    west_side = extended[:, 1:-1, :-2]
    north_side = extended[:, :-2, 1:-1]
    south_side = extended[:, 2:, 1:-1]
    cos_north = cos_all[:-2][:, None]
    cos_south = cos_all[2:][:, None]
    coslat = cos_all[1:-1][:, None]

    def zonal_pair(east_value, west_value):
        return (east_value - west_value) * (0.5 / lon_step)

    def north_pair(north_value, south_value):
        return (north_value - south_value) * (0.5 / lat_step)

    height, east, north = (state[0], state[1], state[2])
    inv_cos = 1.0 / coslat
    turning = 2.0 * OMEGA_RATE * sinlat + east * sinlat * inv_cos
    flux_north = north_side[0] * north_side[2] * cos_north
    flux_south = south_side[0] * south_side[2] * cos_south
    rate_height = (
        -(
            zonal_pair(east_side[0] * east_side[1], west_side[0] * west_side[1])
            + north_pair(flux_north, flux_south)
        )
        * inv_cos
    )
    rate_east = (
        -east * zonal_pair(east_side[1], west_side[1]) * inv_cos
        - north * north_pair(north_side[1], south_side[1])
        + turning * north
        - zonal_pair(east_side[0], west_side[0]) * inv_cos
    )
    rate_north = (
        -east * zonal_pair(east_side[2], west_side[2]) * inv_cos
        - north * north_pair(north_side[2], south_side[2])
        - turning * east
        - north_pair(north_side[0], south_side[0])
    )
    return jnp.stack([rate_height, rate_east, rate_north], axis=0)


def shards(height, east_wind, north_wind, cutoffs):
    rows_here = height.shape[0]
    lat_index = lax.axis_index("lat")
    lat_step = math.pi / LAT_ROWS
    lon_step = 2.0 * math.pi / NLON
    time_step = COURANT * lat_step
    first_row = (lat_index * rows_here).astype(jnp.float32)
    index = first_row + jnp.arange(-1, rows_here + 1).astype(jnp.float32)
    cos_all = jnp.abs(jnp.sin((index + 0.5) * lat_step))
    sin_all = jnp.cos((index + 0.5) * lat_step)
    sinlat = sin_all[1:-1][:, None]
    width = height.shape[1]
    wide_table = local_table(-1, width + 2)
    table = wide_table[:, 1:-1]
    state = jnp.stack([height, east_wind, north_wind], axis=0)
    lon_halos = None
    pole = None
    flips = jnp.array([1.0, -1.0, -1.0], jnp.float32)[:, None]
    for step_index in range(STEPS):
        rates_now = tendency(state, cos_all, sinlat, lon_step, lat_step, lon_halos)
        middle = state + 0.5 * time_step * rates_now
        far = None
        if pole is not None:
            far_wide, near_row = pole
            far_box = jnp.stack([near_row * flips, far_wide[:, 0, :], far_wide[:, 1, :]], axis=1)
            far_rate = rates(far_box, cos_all[0:3], sin_all[1:2], lon_step, lat_step)[:, 0, :]
            far = far_wide[:, 0, 1:-1] + 0.5 * time_step * far_rate
        rates_now = tendency(middle, cos_all, sinlat, lon_step, lat_step, None, far)
        advanced = state + time_step * rates_now
        last = step_index == STEPS - 1
        state, lon_halos, pole = filter_state(advanced, cutoffs, table, wide_table, not last)
    return (state[0], state[1], state[2])


def solution(mesh):
    placed = (P("lat", "lon"), P("lat", "lon"), P("lat", "lon"), P())
    return jax.shard_map(
        shards,
        mesh=mesh,
        in_specs=placed,
        out_specs=(P("lat", "lon"), P("lat", "lon"), P("lat", "lon")),
        check_vma=False,
    )
```

```python
import math

import jax
import jax.numpy as jnp
from jax import lax
from jax.sharding import PartitionSpec as P

NLON = 7200
LAT_ROWS = 3600
KMAX = 64
STEPS = 2


COURANT = 0.1
OMEGA_RATE = 1.5


def with_halo(value, sides, width, wrap):
    for axis, dim in sides:
        devices, length = (lax.axis_size(axis), value.shape[dim])
        up = [(i, (i + 1) % devices) for i in range(devices if wrap else devices - 1)]
        down = [(j, i) for i, j in up]
        last = lax.slice_in_dim(value, length - width, length, axis=dim)
        first = lax.slice_in_dim(value, 0, width, axis=dim)
        before = lax.ppermute(last, axis, up)
        after = lax.ppermute(first, axis, down)
        value = jnp.concatenate([before, value, after], axis=dim)
    return value


def from_behind(value, axis, by):
    devices = lax.axis_size(axis)
    return lax.ppermute(value, axis, [(i, (i + by) % devices) for i in range(devices)])


def local_table(first, width):
    waves = jnp.arange(KMAX + 1, dtype=jnp.int32)
    columns = (lax.axis_index("lon") * NLON // lax.axis_size("lon") + first) % NLON
    columns = (columns + jnp.arange(width, dtype=jnp.int32)) % NLON
    phase = waves[:, None] * columns[None, :] % NLON
    angle = phase.astype(jnp.float32) * (2.0 * math.pi / NLON)
    return jnp.concatenate([jnp.cos(angle), jnp.sin(angle)], axis=0)


def spectral_weights(cut_rows):
    waves = jnp.arange(KMAX + 1, dtype=jnp.int32)
    scale = jnp.where(waves == 0, 1.0 / NLON, 2.0 / NLON).astype(jnp.float32)
    keep = (waves[None, :] <= cut_rows[:, None]).astype(jnp.float32) * scale[None, :]
    return jnp.concatenate([keep, keep], axis=1)


def half_turn_signs():
    waves = jnp.arange(KMAX + 1, dtype=jnp.int32)
    signs = jnp.where(waves % 2 == 0, 1.0, -1.0).astype(jnp.float32)
    return jnp.concatenate([signs, signs], axis=0)


def project(fields, table):
    return jnp.einsum("fnw,kw->fnk", fields, table, precision=lax.Precision.HIGH)


def expand(coeffs, table):
    return jnp.einsum("fnk,kw->fnw", coeffs, table, precision=lax.Precision.HIGH)


def low_pass(fields, cut_rows, active, table, wide_table, with_halos):
    devices = lax.axis_size("lon")
    lon_index = lax.axis_index("lon")
    count, rows, width = fields.shape
    share = rows // devices
    partial = project(fields, table)
    modes = partial.shape[2]
    gathered = lax.all_to_all(partial, "lon", split_axis=1, concat_axis=0, tiled=True)
    reduced = gathered.reshape(devices, count, share, modes).sum(axis=0)
    payload = [jnp.broadcast_to(reduced.reshape(1, -1), (devices, count * share * modes))]
    if with_halos:
        targets = jnp.arange(devices, dtype=jnp.int32)[:, None]
        to_east = targets == (lon_index + 1) % devices
        edge = jnp.where(to_east, fields[:, :, -1].reshape(1, -1), fields[:, :, 0].reshape(1, -1))
        payload += [edge, jnp.broadcast_to(fields[:, 0, :].reshape(1, -1), (devices, count * width))]
    spread = lax.all_to_all(jnp.concatenate(payload, axis=1), "lon", split_axis=0, concat_axis=0, tiled=True)
    block = count * share * modes
    coeffs = spread[:, :block].reshape(devices, count, share, modes)
    coeffs = jnp.moveaxis(coeffs, 0, 1).reshape(count, rows, modes)
    weights = spectral_weights(cut_rows)
    scaled = coeffs * weights[None]
    if not with_halos:
        smooth = expand(scaled, table)
        return jnp.where(active[None, :, None], smooth, fields), None, None
    pole_coeffs = scaled[:, :2, :] * half_turn_signs()[None, None, :]
    both = expand(jnp.concatenate([scaled, pole_coeffs], axis=1), wide_table)
    wide = both[:, :rows, :]
    smooth = wide[:, :, 1:-1]
    filtered = jnp.where(active[None, :, None], smooth, fields)
    edges = spread[:, block:block + count * rows].reshape(devices, count, rows)
    rows_far = spread[:, block + count * rows:].reshape(devices, count, width)
    west_raw = edges[(lon_index - 1) % devices]
    east_raw = edges[(lon_index + 1) % devices]
    far_raw = rows_far[(lon_index + devices // 2) % devices]
    west = jnp.where(active[None, :], wide[:, :, 0], west_raw)[:, :, None]
    east = jnp.where(active[None, :], wide[:, :, -1], east_raw)[:, :, None]
    far_wide = both[:, rows:, :]
    far = jnp.where(active[0], far_wide[:, 0, 1:-1], far_raw)
    return filtered, (west, east, far), (far_wide, wide[:, 0, :])


def filter_state(state, cutoffs, table, wide_table, with_halos):
    rows_here = state.shape[1]
    lat_count = lax.axis_size("lat")
    lat_index = lax.axis_index("lat")
    filtered_rows = cutoffs.shape[0]
    cut_all = jnp.pad(cutoffs, (0, rows_here * lat_count - filtered_rows))
    global_rows = lat_index * rows_here + jnp.arange(rows_here, dtype=jnp.int32)
    cut_rows = lax.dynamic_slice_in_dim(cut_all, lat_index * rows_here, rows_here, 0)
    return low_pass(state, cut_rows, global_rows < filtered_rows, table, wide_table, with_halos)


def rates(ext, cos_all, sinlat, lon_step, lat_step):
    east_side = ext[:, 1:-1, 2:]
    west_side = ext[:, 1:-1, :-2]
    north_side = ext[:, :-2, 1:-1]
    south_side = ext[:, 2:, 1:-1]
    cos_north = cos_all[:-2][:, None]
    cos_south = cos_all[2:][:, None]
    coslat = cos_all[1:-1][:, None]
    sinlat = sinlat[:, None]

    def zonal_pair(east_value, west_value):
        return (east_value - west_value) * (0.5 / lon_step)

    def north_pair(north_value, south_value):
        return (north_value - south_value) * (0.5 / lat_step)

    centre = ext[:, 1:-1, 1:-1]
    height, east, north = (centre[0], centre[1], centre[2])
    inv_cos = 1.0 / coslat
    turning = 2.0 * OMEGA_RATE * sinlat + east * sinlat * inv_cos
    flux_north = north_side[0] * north_side[2] * cos_north
    flux_south = south_side[0] * south_side[2] * cos_south
    rate_height = (
        -(
            zonal_pair(east_side[0] * east_side[1], west_side[0] * west_side[1])
            + north_pair(flux_north, flux_south)
        )
        * inv_cos
    )
    rate_east = (
        -east * zonal_pair(east_side[1], west_side[1]) * inv_cos
        - north * north_pair(north_side[1], south_side[1])
        + turning * north
        - zonal_pair(east_side[0], west_side[0]) * inv_cos
    )
    rate_north = (
        -east * zonal_pair(east_side[2], west_side[2]) * inv_cos
        - north * north_pair(north_side[2], south_side[2])
        - turning * east
        - north_pair(north_side[0], south_side[0])
    )
    return jnp.stack([rate_height, rate_east, rate_north], axis=0)


def tendency(state, cos_all, sinlat, lon_step, lat_step, lon_halos=None, far=None):
    lat_index = lax.axis_index("lat")
    lat_count = lax.axis_size("lat")
    flips = jnp.array([1.0, -1.0, -1.0], jnp.float32)
    if lon_halos is None:
        edge_cols = jnp.concatenate([state[:, :, :1], state[:, :, -1:]], axis=2)
        got_cols = with_halo(edge_cols, (("lon", 2),), 1, True)
        west_col = got_cols[:, :, 0:1]
        east_col = got_cols[:, :, 3:4]
        if far is None:
            mirror = from_behind(state[:, 0, :], "lon", lax.axis_size("lon") // 2)
        else:
            mirror = far
    else:
        west_col, east_col, mirror = lon_halos
    mirror = mirror * flips[:, None]
    edge_rows = jnp.concatenate([state[:, :1, :], state[:, -1:, :]], axis=1)
    got_rows = with_halo(edge_rows, (("lat", 1),), 1, False)
    northmost = jnp.where(lat_index == 0, mirror, got_rows[:, 0, :])
    southmost = jnp.where(lat_index == lat_count - 1, state[:, -1, :], got_rows[:, 3, :])
    corner = jnp.zeros((3, 1, 1), jnp.float32)
    top_line = jnp.concatenate([corner, northmost[:, None, :], corner], axis=2)
    bottom_line = jnp.concatenate([corner, southmost[:, None, :], corner], axis=2)
    middle_lines = jnp.concatenate([west_col, state, east_col], axis=2)
    extended = jnp.concatenate([top_line, middle_lines, bottom_line], axis=1)
    east_side = extended[:, 1:-1, 2:]
    west_side = extended[:, 1:-1, :-2]
    north_side = extended[:, :-2, 1:-1]
    south_side = extended[:, 2:, 1:-1]
    cos_north = cos_all[:-2][:, None]
    cos_south = cos_all[2:][:, None]
    coslat = cos_all[1:-1][:, None]

    def zonal_pair(east_value, west_value):
        return (east_value - west_value) * (0.5 / lon_step)

    def north_pair(north_value, south_value):
        return (north_value - south_value) * (0.5 / lat_step)

    height, east, north = (state[0], state[1], state[2])
    inv_cos = 1.0 / coslat
    turning = 2.0 * OMEGA_RATE * sinlat + east * sinlat * inv_cos
    flux_north = north_side[0] * north_side[2] * cos_north
    flux_south = south_side[0] * south_side[2] * cos_south
    rate_height = (
        -(
            zonal_pair(east_side[0] * east_side[1], west_side[0] * west_side[1])
            + north_pair(flux_north, flux_south)
        )
        * inv_cos
    )
    rate_east = (
        -east * zonal_pair(east_side[1], west_side[1]) * inv_cos
        - north * north_pair(north_side[1], south_side[1])
        + turning * north
        - zonal_pair(east_side[0], west_side[0]) * inv_cos
    )
    rate_north = (
        -east * zonal_pair(east_side[2], west_side[2]) * inv_cos
        - north * north_pair(north_side[2], south_side[2])
        - turning * east
        - north_pair(north_side[0], south_side[0])
    )
    return jnp.stack([rate_height, rate_east, rate_north], axis=0)


def shards(height, east_wind, north_wind, cutoffs):
    rows_here = height.shape[0]
    lat_index = lax.axis_index("lat")
    lat_step = math.pi / LAT_ROWS
    lon_step = 2.0 * math.pi / NLON
    time_step = COURANT * lat_step
    first_row = (lat_index * rows_here).astype(jnp.float32)
    index = first_row + jnp.arange(-1, rows_here + 1).astype(jnp.float32)
    cos_all = jnp.abs(jnp.sin((index + 0.5) * lat_step))
    sin_all = jnp.cos((index + 0.5) * lat_step)
    sinlat = sin_all[1:-1][:, None]
    width = height.shape[1]
    table = local_table(0, width)
    wide_table = local_table(-1, width + 2)
    state = jnp.stack([height, east_wind, north_wind], axis=0)
    lon_halos = None
    pole = None
    flips = jnp.array([1.0, -1.0, -1.0], jnp.float32)[:, None]
    for step_index in range(STEPS):
        rates_now = tendency(state, cos_all, sinlat, lon_step, lat_step, lon_halos)
        middle = state + 0.5 * time_step * rates_now
        far = None
        if pole is not None:
            far_wide, near_row = pole
            far_box = jnp.stack([near_row * flips, far_wide[:, 0, :], far_wide[:, 1, :]], axis=1)
            far_rate = rates(far_box, cos_all[0:3], sin_all[1:2], lon_step, lat_step)[:, 0, :]
            far = far_wide[:, 0, 1:-1] + 0.5 * time_step * far_rate
        rates_now = tendency(middle, cos_all, sinlat, lon_step, lat_step, None, far)
        advanced = state + time_step * rates_now
        last = step_index == STEPS - 1
        state, lon_halos, pole = filter_state(advanced, cutoffs, table, wide_table, not last)
    return (state[0], state[1], state[2])


def solution(mesh):
    placed = (P("lat", "lon"), P("lat", "lon"), P("lat", "lon"), P())
    return jax.shard_map(
        shards,
        mesh=mesh,
        in_specs=placed,
        out_specs=(P("lat", "lon"), P("lat", "lon"), P("lat", "lon")),
        check_vma=False,
    )
```

```python
import math

import jax
import jax.numpy as jnp
from jax import lax
from jax.sharding import PartitionSpec as P

NLON = 7200
LAT_ROWS = 3600
KMAX = 64
STEPS = 2


COURANT = 0.1
OMEGA_RATE = 1.5


def with_halo(value, sides, width, wrap):
    for axis, dim in sides:
        devices, length = (lax.axis_size(axis), value.shape[dim])
        up = [(i, (i + 1) % devices) for i in range(devices if wrap else devices - 1)]
        down = [(j, i) for i, j in up]
        last = lax.slice_in_dim(value, length - width, length, axis=dim)
        first = lax.slice_in_dim(value, 0, width, axis=dim)
        before = lax.ppermute(last, axis, up)
        after = lax.ppermute(first, axis, down)
        value = jnp.concatenate([before, value, after], axis=dim)
    return value


def from_behind(value, axis, by):
    devices = lax.axis_size(axis)
    return lax.ppermute(value, axis, [(i, (i + by) % devices) for i in range(devices)])


def local_table(first, width):
    waves = jnp.arange(KMAX + 1, dtype=jnp.int32)
    columns = (lax.axis_index("lon") * NLON // lax.axis_size("lon") + first) % NLON
    columns = (columns + jnp.arange(width, dtype=jnp.int32)) % NLON
    phase = waves[:, None] * columns[None, :] % NLON
    angle = phase.astype(jnp.float32) * (2.0 * math.pi / NLON)
    return jnp.concatenate([jnp.cos(angle), jnp.sin(angle)], axis=0)


def spectral_weights(cut_rows):
    waves = jnp.arange(KMAX + 1, dtype=jnp.int32)
    scale = jnp.where(waves == 0, 1.0 / NLON, 2.0 / NLON).astype(jnp.float32)
    keep = (waves[None, :] <= cut_rows[:, None]).astype(jnp.float32) * scale[None, :]
    return jnp.concatenate([keep, keep], axis=1)


def half_turn_signs():
    waves = jnp.arange(KMAX + 1, dtype=jnp.int32)
    signs = jnp.where(waves % 2 == 0, 1.0, -1.0).astype(jnp.float32)
    return jnp.concatenate([signs, signs], axis=0)


def project(fields, table):
    return jnp.einsum("fnw,kw->fnk", fields, table, precision=lax.Precision.HIGH)


def expand(coeffs, table):
    return jnp.einsum("fnk,kw->fnw", coeffs, table, precision=lax.Precision.HIGH)


def low_pass(fields, cut_rows, active, table, wide_table, with_halos):
    devices = lax.axis_size("lon")
    lon_index = lax.axis_index("lon")
    count, rows, width = fields.shape
    share = rows // devices
    partial = project(fields, table)
    modes = partial.shape[2]
    gathered = lax.all_to_all(partial, "lon", split_axis=1, concat_axis=0, tiled=True)
    reduced = gathered.reshape(devices, count, share, modes).sum(axis=0)
    payload = [jnp.broadcast_to(reduced.reshape(1, -1), (devices, count * share * modes))]
    if with_halos:
        targets = jnp.arange(devices, dtype=jnp.int32)[:, None]
        to_east = targets == (lon_index + 1) % devices
        edge = jnp.where(to_east, fields[:, :, -1].reshape(1, -1), fields[:, :, 0].reshape(1, -1))
        payload += [edge]
    spread = lax.all_to_all(jnp.concatenate(payload, axis=1), "lon", split_axis=0, concat_axis=0, tiled=True)
    block = count * share * modes
    coeffs = spread[:, :block].reshape(devices, count, share, modes)
    coeffs = jnp.moveaxis(coeffs, 0, 1).reshape(count, rows, modes)
    weights = spectral_weights(cut_rows)
    scaled = coeffs * weights[None]
    if not with_halos:
        smooth = expand(scaled, table)
        return jnp.where(active[None, :, None], smooth, fields), None, None
    wide = expand(scaled, wide_table)
    smooth = wide[:, :, 1:-1]
    filtered = jnp.where(active[None, :, None], smooth, fields)
    edges = spread[:, block:].reshape(devices, count, rows)
    west_raw = edges[(lon_index - 1) % devices]
    east_raw = edges[(lon_index + 1) % devices]
    west = jnp.where(active[None, :], wide[:, :, 0], west_raw)[:, :, None]
    east = jnp.where(active[None, :], wide[:, :, -1], east_raw)[:, :, None]
    far_wide = expand(scaled[:, :2, :] * half_turn_signs()[None, None, :], wide_table)
    far = far_wide[:, 0, 1:-1]
    return filtered, (west, east, far), (far_wide, wide[:, 0, :])


def filter_state(state, cutoffs, table, wide_table, with_halos):
    rows_here = state.shape[1]
    lat_count = lax.axis_size("lat")
    lat_index = lax.axis_index("lat")
    filtered_rows = cutoffs.shape[0]
    cut_all = jnp.pad(cutoffs, (0, rows_here * lat_count - filtered_rows))
    global_rows = lat_index * rows_here + jnp.arange(rows_here, dtype=jnp.int32)
    cut_rows = lax.dynamic_slice_in_dim(cut_all, lat_index * rows_here, rows_here, 0)
    return low_pass(state, cut_rows, global_rows < filtered_rows, table, wide_table, with_halos)


def rates(ext, cos_all, sinlat, lon_step, lat_step):
    east_side = ext[:, 1:-1, 2:]
    west_side = ext[:, 1:-1, :-2]
    north_side = ext[:, :-2, 1:-1]
    south_side = ext[:, 2:, 1:-1]
    cos_north = cos_all[:-2][:, None]
    cos_south = cos_all[2:][:, None]
    coslat = cos_all[1:-1][:, None]
    sinlat = sinlat[:, None]

    def zonal_pair(east_value, west_value):
        return (east_value - west_value) * (0.5 / lon_step)

    def north_pair(north_value, south_value):
        return (north_value - south_value) * (0.5 / lat_step)

    centre = ext[:, 1:-1, 1:-1]
    height, east, north = (centre[0], centre[1], centre[2])
    inv_cos = 1.0 / coslat
    turning = 2.0 * OMEGA_RATE * sinlat + east * sinlat * inv_cos
    flux_north = north_side[0] * north_side[2] * cos_north
    flux_south = south_side[0] * south_side[2] * cos_south
    rate_height = (
        -(
            zonal_pair(east_side[0] * east_side[1], west_side[0] * west_side[1])
            + north_pair(flux_north, flux_south)
        )
        * inv_cos
    )
    rate_east = (
        -east * zonal_pair(east_side[1], west_side[1]) * inv_cos
        - north * north_pair(north_side[1], south_side[1])
        + turning * north
        - zonal_pair(east_side[0], west_side[0]) * inv_cos
    )
    rate_north = (
        -east * zonal_pair(east_side[2], west_side[2]) * inv_cos
        - north * north_pair(north_side[2], south_side[2])
        - turning * east
        - north_pair(north_side[0], south_side[0])
    )
    return jnp.stack([rate_height, rate_east, rate_north], axis=0)


def tendency(state, cos_all, sinlat, lon_step, lat_step, lon_halos=None, far=None):
    lat_index = lax.axis_index("lat")
    lat_count = lax.axis_size("lat")
    flips = jnp.array([1.0, -1.0, -1.0], jnp.float32)
    if lon_halos is None:
        edge_cols = jnp.concatenate([state[:, :, :1], state[:, :, -1:]], axis=2)
        got_cols = with_halo(edge_cols, (("lon", 2),), 1, True)
        west_col = got_cols[:, :, 0:1]
        east_col = got_cols[:, :, 3:4]
        if far is None:
            mirror = from_behind(state[:, 0, :], "lon", lax.axis_size("lon") // 2)
        else:
            mirror = far
    else:
        west_col, east_col, mirror = lon_halos
    mirror = mirror * flips[:, None]
    edge_rows = jnp.concatenate([state[:, :1, :], state[:, -1:, :]], axis=1)
    got_rows = with_halo(edge_rows, (("lat", 1),), 1, False)
    northmost = jnp.where(lat_index == 0, mirror, got_rows[:, 0, :])
    southmost = jnp.where(lat_index == lat_count - 1, state[:, -1, :], got_rows[:, 3, :])
    corner = jnp.zeros((3, 1, 1), jnp.float32)
    top_line = jnp.concatenate([corner, northmost[:, None, :], corner], axis=2)
    bottom_line = jnp.concatenate([corner, southmost[:, None, :], corner], axis=2)
    middle_lines = jnp.concatenate([west_col, state, east_col], axis=2)
    extended = jnp.concatenate([top_line, middle_lines, bottom_line], axis=1)
    east_side = extended[:, 1:-1, 2:]
    west_side = extended[:, 1:-1, :-2]
    north_side = extended[:, :-2, 1:-1]
    south_side = extended[:, 2:, 1:-1]
    cos_north = cos_all[:-2][:, None]
    cos_south = cos_all[2:][:, None]
    coslat = cos_all[1:-1][:, None]

    def zonal_pair(east_value, west_value):
        return (east_value - west_value) * (0.5 / lon_step)

    def north_pair(north_value, south_value):
        return (north_value - south_value) * (0.5 / lat_step)

    height, east, north = (state[0], state[1], state[2])
    inv_cos = 1.0 / coslat
    turning = 2.0 * OMEGA_RATE * sinlat + east * sinlat * inv_cos
    flux_north = north_side[0] * north_side[2] * cos_north
    flux_south = south_side[0] * south_side[2] * cos_south
    rate_height = (
        -(
            zonal_pair(east_side[0] * east_side[1], west_side[0] * west_side[1])
            + north_pair(flux_north, flux_south)
        )
        * inv_cos
    )
    rate_east = (
        -east * zonal_pair(east_side[1], west_side[1]) * inv_cos
        - north * north_pair(north_side[1], south_side[1])
        + turning * north
        - zonal_pair(east_side[0], west_side[0]) * inv_cos
    )
    rate_north = (
        -east * zonal_pair(east_side[2], west_side[2]) * inv_cos
        - north * north_pair(north_side[2], south_side[2])
        - turning * east
        - north_pair(north_side[0], south_side[0])
    )
    return jnp.stack([rate_height, rate_east, rate_north], axis=0)


def shards(height, east_wind, north_wind, cutoffs):
    rows_here = height.shape[0]
    lat_index = lax.axis_index("lat")
    lat_step = math.pi / LAT_ROWS
    lon_step = 2.0 * math.pi / NLON
    time_step = COURANT * lat_step
    first_row = (lat_index * rows_here).astype(jnp.float32)
    index = first_row + jnp.arange(-1, rows_here + 1).astype(jnp.float32)
    cos_all = jnp.abs(jnp.sin((index + 0.5) * lat_step))
    sin_all = jnp.cos((index + 0.5) * lat_step)
    sinlat = sin_all[1:-1][:, None]
    width = height.shape[1]
    table = local_table(0, width)
    wide_table = local_table(-1, width + 2)
    state = jnp.stack([height, east_wind, north_wind], axis=0)
    lon_halos = None
    pole = None
    flips = jnp.array([1.0, -1.0, -1.0], jnp.float32)[:, None]
    for step_index in range(STEPS):
        rates_now = tendency(state, cos_all, sinlat, lon_step, lat_step, lon_halos)
        middle = state + 0.5 * time_step * rates_now
        far = None
        if pole is not None:
            far_wide, near_row = pole
            far_box = jnp.stack([near_row * flips, far_wide[:, 0, :], far_wide[:, 1, :]], axis=1)
            far_rate = rates(far_box, cos_all[0:3], sin_all[1:2], lon_step, lat_step)[:, 0, :]
            far = far_wide[:, 0, 1:-1] + 0.5 * time_step * far_rate
        rates_now = tendency(middle, cos_all, sinlat, lon_step, lat_step, None, far)
        advanced = state + time_step * rates_now
        last = step_index == STEPS - 1
        state, lon_halos, pole = filter_state(advanced, cutoffs, table, wide_table, not last)
    return (state[0], state[1], state[2])


def solution(mesh):
    placed = (P("lat", "lon"), P("lat", "lon"), P("lat", "lon"), P())
    return jax.shard_map(
        shards,
        mesh=mesh,
        in_specs=placed,
        out_specs=(P("lat", "lon"), P("lat", "lon"), P("lat", "lon")),
        check_vma=False,
    )
```

```python
import math

import jax
import jax.numpy as jnp
from jax import lax
from jax.sharding import PartitionSpec as P

NLON = 7200
LAT_ROWS = 3600
KMAX = 64
STEPS = 2


COURANT = 0.1
OMEGA_RATE = 1.5


def with_halo(value, sides, width, wrap):
    for axis, dim in sides:
        devices, length = (lax.axis_size(axis), value.shape[dim])
        up = [(i, (i + 1) % devices) for i in range(devices if wrap else devices - 1)]
        down = [(j, i) for i, j in up]
        last = lax.slice_in_dim(value, length - width, length, axis=dim)
        first = lax.slice_in_dim(value, 0, width, axis=dim)
        before = lax.ppermute(last, axis, up)
        after = lax.ppermute(first, axis, down)
        value = jnp.concatenate([before, value, after], axis=dim)
    return value


def from_behind(value, axis, by):
    devices = lax.axis_size(axis)
    return lax.ppermute(value, axis, [(i, (i + by) % devices) for i in range(devices)])


def local_table(first, width):
    waves = jnp.arange(KMAX + 1, dtype=jnp.int32)
    columns = (lax.axis_index("lon") * NLON // lax.axis_size("lon") + first) % NLON
    columns = (columns + jnp.arange(width, dtype=jnp.int32)) % NLON
    phase = waves[:, None] * columns[None, :] % NLON
    angle = phase.astype(jnp.float32) * (2.0 * math.pi / NLON)
    return jnp.concatenate([jnp.cos(angle), jnp.sin(angle)], axis=0)


def spectral_weights(cut_rows):
    waves = jnp.arange(KMAX + 1, dtype=jnp.int32)
    scale = jnp.where(waves == 0, 1.0 / NLON, 2.0 / NLON).astype(jnp.float32)
    keep = (waves[None, :] <= cut_rows[:, None]).astype(jnp.float32) * scale[None, :]
    return jnp.concatenate([keep, keep], axis=1)


def half_turn_signs():
    waves = jnp.arange(KMAX + 1, dtype=jnp.int32)
    signs = jnp.where(waves % 2 == 0, 1.0, -1.0).astype(jnp.float32)
    return jnp.concatenate([signs, signs], axis=0)


def project(fields, table):
    return jnp.einsum("fnw,kw->fnk", fields, table, precision=lax.Precision.HIGH)


def expand(coeffs, table):
    return jnp.einsum("fnk,kw->fnw", coeffs, table, precision=lax.Precision.HIGH)


def low_pass(fields, cut_rows, active, table, wide_table, with_halos):
    devices = lax.axis_size("lon")
    lon_index = lax.axis_index("lon")
    count, rows, width = fields.shape
    share = rows // devices
    partial = jnp.einsum("fnw,kw->nfk", fields, table, precision=lax.Precision.HIGH)
    modes = partial.shape[2]
    gathered = lax.all_to_all(partial, "lon", split_axis=0, concat_axis=0, tiled=True)
    reduced = gathered.reshape(devices, share, count, modes).sum(axis=0)
    payload = [jnp.broadcast_to(reduced.reshape(1, -1), (devices, count * share * modes))]
    if with_halos:
        targets = jnp.arange(devices, dtype=jnp.int32)[:, None]
        to_east = targets == (lon_index + 1) % devices
        edge = jnp.where(to_east, fields[:, :, -1].reshape(1, -1), fields[:, :, 0].reshape(1, -1))
        payload += [edge, jnp.broadcast_to(fields[:, 0, :].reshape(1, -1), (devices, count * width))]
    spread = lax.all_to_all(jnp.concatenate(payload, axis=1), "lon", split_axis=0, concat_axis=0, tiled=True)
    block = count * share * modes
    coeffs = spread[:, :block].reshape(devices, share, count, modes)
    coeffs = coeffs.transpose(2, 0, 1, 3).reshape(count, rows, modes)
    weights = spectral_weights(cut_rows)
    scaled = coeffs * weights[None]
    if not with_halos:
        smooth = expand(scaled, table)
        return jnp.where(active[None, :, None], smooth, fields), None, None
    wide = expand(scaled, wide_table)
    smooth = wide[:, :, 1:-1]
    filtered = jnp.where(active[None, :, None], smooth, fields)
    edges = spread[:, block:block + count * rows].reshape(devices, count, rows)
    rows_far = spread[:, block + count * rows:].reshape(devices, count, width)
    west_raw = edges[(lon_index - 1) % devices]
    east_raw = edges[(lon_index + 1) % devices]
    far_raw = rows_far[(lon_index + devices // 2) % devices]
    west = jnp.where(active[None, :], wide[:, :, 0], west_raw)[:, :, None]
    east = jnp.where(active[None, :], wide[:, :, -1], east_raw)[:, :, None]
    far_wide = expand(scaled[:, :2, :] * half_turn_signs()[None, None, :], wide_table)
    far = jnp.where(active[0], far_wide[:, 0, 1:-1], far_raw)
    return filtered, (west, east, far), (far_wide, wide[:, 0, :])


def filter_state(state, cutoffs, table, wide_table, with_halos):
    rows_here = state.shape[1]
    lat_count = lax.axis_size("lat")
    lat_index = lax.axis_index("lat")
    filtered_rows = cutoffs.shape[0]
    cut_all = jnp.pad(cutoffs, (0, rows_here * lat_count - filtered_rows))
    global_rows = lat_index * rows_here + jnp.arange(rows_here, dtype=jnp.int32)
    cut_rows = lax.dynamic_slice_in_dim(cut_all, lat_index * rows_here, rows_here, 0)
    return low_pass(state, cut_rows, global_rows < filtered_rows, table, wide_table, with_halos)


def rates(ext, cos_all, sinlat, lon_step, lat_step):
    east_side = ext[:, 1:-1, 2:]
    west_side = ext[:, 1:-1, :-2]
    north_side = ext[:, :-2, 1:-1]
    south_side = ext[:, 2:, 1:-1]
    cos_north = cos_all[:-2][:, None]
    cos_south = cos_all[2:][:, None]
    coslat = cos_all[1:-1][:, None]
    sinlat = sinlat[:, None]

    def zonal_pair(east_value, west_value):
        return (east_value - west_value) * (0.5 / lon_step)

    def north_pair(north_value, south_value):
        return (north_value - south_value) * (0.5 / lat_step)

    centre = ext[:, 1:-1, 1:-1]
    height, east, north = (centre[0], centre[1], centre[2])
    inv_cos = 1.0 / coslat
    turning = 2.0 * OMEGA_RATE * sinlat + east * sinlat * inv_cos
    flux_north = north_side[0] * north_side[2] * cos_north
    flux_south = south_side[0] * south_side[2] * cos_south
    rate_height = (
        -(
            zonal_pair(east_side[0] * east_side[1], west_side[0] * west_side[1])
            + north_pair(flux_north, flux_south)
        )
        * inv_cos
    )
    rate_east = (
        -east * zonal_pair(east_side[1], west_side[1]) * inv_cos
        - north * north_pair(north_side[1], south_side[1])
        + turning * north
        - zonal_pair(east_side[0], west_side[0]) * inv_cos
    )
    rate_north = (
        -east * zonal_pair(east_side[2], west_side[2]) * inv_cos
        - north * north_pair(north_side[2], south_side[2])
        - turning * east
        - north_pair(north_side[0], south_side[0])
    )
    return jnp.stack([rate_height, rate_east, rate_north], axis=0)


def tendency(state, cos_all, sinlat, lon_step, lat_step, lon_halos=None, far=None):
    lat_index = lax.axis_index("lat")
    lat_count = lax.axis_size("lat")
    flips = jnp.array([1.0, -1.0, -1.0], jnp.float32)
    if lon_halos is None:
        edge_cols = jnp.concatenate([state[:, :, :1], state[:, :, -1:]], axis=2)
        got_cols = with_halo(edge_cols, (("lon", 2),), 1, True)
        west_col = got_cols[:, :, 0:1]
        east_col = got_cols[:, :, 3:4]
        if far is None:
            mirror = from_behind(state[:, 0, :], "lon", lax.axis_size("lon") // 2)
        else:
            mirror = far
    else:
        west_col, east_col, mirror = lon_halos
    mirror = mirror * flips[:, None]
    edge_rows = jnp.concatenate([state[:, :1, :], state[:, -1:, :]], axis=1)
    got_rows = with_halo(edge_rows, (("lat", 1),), 1, False)
    northmost = jnp.where(lat_index == 0, mirror, got_rows[:, 0, :])
    southmost = jnp.where(lat_index == lat_count - 1, state[:, -1, :], got_rows[:, 3, :])
    corner = jnp.zeros((3, 1, 1), jnp.float32)
    top_line = jnp.concatenate([corner, northmost[:, None, :], corner], axis=2)
    bottom_line = jnp.concatenate([corner, southmost[:, None, :], corner], axis=2)
    middle_lines = jnp.concatenate([west_col, state, east_col], axis=2)
    extended = jnp.concatenate([top_line, middle_lines, bottom_line], axis=1)
    east_side = extended[:, 1:-1, 2:]
    west_side = extended[:, 1:-1, :-2]
    north_side = extended[:, :-2, 1:-1]
    south_side = extended[:, 2:, 1:-1]
    cos_north = cos_all[:-2][:, None]
    cos_south = cos_all[2:][:, None]
    coslat = cos_all[1:-1][:, None]

    def zonal_pair(east_value, west_value):
        return (east_value - west_value) * (0.5 / lon_step)

    def north_pair(north_value, south_value):
        return (north_value - south_value) * (0.5 / lat_step)

    height, east, north = (state[0], state[1], state[2])
    inv_cos = 1.0 / coslat
    turning = 2.0 * OMEGA_RATE * sinlat + east * sinlat * inv_cos
    flux_north = north_side[0] * north_side[2] * cos_north
    flux_south = south_side[0] * south_side[2] * cos_south
    rate_height = (
        -(
            zonal_pair(east_side[0] * east_side[1], west_side[0] * west_side[1])
            + north_pair(flux_north, flux_south)
        )
        * inv_cos
    )
    rate_east = (
        -east * zonal_pair(east_side[1], west_side[1]) * inv_cos
        - north * north_pair(north_side[1], south_side[1])
        + turning * north
        - zonal_pair(east_side[0], west_side[0]) * inv_cos
    )
    rate_north = (
        -east * zonal_pair(east_side[2], west_side[2]) * inv_cos
        - north * north_pair(north_side[2], south_side[2])
        - turning * east
        - north_pair(north_side[0], south_side[0])
    )
    return jnp.stack([rate_height, rate_east, rate_north], axis=0)


def shards(height, east_wind, north_wind, cutoffs):
    rows_here = height.shape[0]
    lat_index = lax.axis_index("lat")
    lat_step = math.pi / LAT_ROWS
    lon_step = 2.0 * math.pi / NLON
    time_step = COURANT * lat_step
    first_row = (lat_index * rows_here).astype(jnp.float32)
    index = first_row + jnp.arange(-1, rows_here + 1).astype(jnp.float32)
    cos_all = jnp.abs(jnp.sin((index + 0.5) * lat_step))
    sin_all = jnp.cos((index + 0.5) * lat_step)
    sinlat = sin_all[1:-1][:, None]
    width = height.shape[1]
    table = local_table(0, width)
    wide_table = local_table(-1, width + 2)
    state = jnp.stack([height, east_wind, north_wind], axis=0)
    lon_halos = None
    pole = None
    flips = jnp.array([1.0, -1.0, -1.0], jnp.float32)[:, None]
    for step_index in range(STEPS):
        rates_now = tendency(state, cos_all, sinlat, lon_step, lat_step, lon_halos)
        middle = state + 0.5 * time_step * rates_now
        far = None
        if pole is not None:
            far_wide, near_row = pole
            far_box = jnp.stack([near_row * flips, far_wide[:, 0, :], far_wide[:, 1, :]], axis=1)
            far_rate = rates(far_box, cos_all[0:3], sin_all[1:2], lon_step, lat_step)[:, 0, :]
            far = far_wide[:, 0, 1:-1] + 0.5 * time_step * far_rate
        rates_now = tendency(middle, cos_all, sinlat, lon_step, lat_step, None, far)
        advanced = state + time_step * rates_now
        last = step_index == STEPS - 1
        state, lon_halos, pole = filter_state(advanced, cutoffs, table, wide_table, not last)
    return (state[0], state[1], state[2])


def solution(mesh):
    placed = (P("lat", "lon"), P("lat", "lon"), P("lat", "lon"), P())
    return jax.shard_map(
        shards,
        mesh=mesh,
        in_specs=placed,
        out_specs=(P("lat", "lon"), P("lat", "lon"), P("lat", "lon")),
        check_vma=False,
    )
```
